128 devices in a mesh: heads: 8 (over y, core), seq: 16 (over z, x).
Axes of the slice: x: 4, y: 4, z: 4, core: 2. Of those that a mesh axis runs over, the one named last changes fastest.
Arguments:
- queries: bfloat16 [8192, 32768], P(('heads', 'seq')), may hold values from -84 to 84
- keys: bfloat16 [8192, 32768], P(('heads', 'seq')), may hold values from -6 to 6
- values: bfloat16 [8192, 32768], P(('heads', 'seq')), may hold values from -12 to 12
- feat_q: bfloat16 [64, 128, 64], P('heads'), may hold values from -3 to 3
- feat_k: bfloat16 [64, 128, 64], P('heads'), may hold values from -3 to 3
- mix: float32 [64], P('heads'), may hold values from -2 to 2
Outputs:
- attended: bfloat16 [32768, 8192], P('seq', 'heads')
The draws below stay inside these ranges and needn't reach their ends.
All inputs are finite; a program needn't handle non-finite values.
Results may differ from the reference program's by a relative error of at most 0.0054.
Values may be sent and summed in bfloat16 or wider, within the bound.
No kernel may reach another device: no remote copies, remote signals or barrier semaphores. Data moves between devices by JAX's collectives and lax.ppermute only.
A program may use at most 128 MiB of HBM per device.

```python
import jax
import jax.numpy as jnp
from jax import lax

H = 64
HD = 128
HF = 64
WIN = 64
L_DEV = 2048
BLOCK = 512
TOKENS = 32768


def paired_rows(key):
    base = jax.random.fold_in(key, 7)
    key_query, key_key = jax.random.split(base)
    shape = (TOKENS, H * HD)
    query_out = jnp.clip(jax.random.normal(key_query, shape, jnp.float32), -6.0, 6.0)
    key_out = jnp.clip(jax.random.normal(key_key, shape, jnp.float32), -6.0, 6.0)
    return (query_out, key_out)


def draw_queries(key, part):
    return paired_rows(key)[0].T.astype(jnp.bfloat16)


def draw_keys(key, part):
    return paired_rows(key)[1].T.astype(jnp.bfloat16)


def draw_values(key, part):
    key_noise, key_offset, key_sign = jax.random.split(jax.random.fold_in(key, 13), 3)
    regions = TOKENS // L_DEV
    shape = (TOKENS, H * HD)
    key_part = paired_rows(key)[1].astype(jnp.bfloat16).astype(jnp.float32)
    signs = jax.random.rademacher(key_sign, (H * HD,), jnp.float32)
    linked = jnp.roll(key_part, 1, axis=1) * signs[None, :]
    noise = jnp.clip(jax.random.normal(key_noise, shape, jnp.float32), -6.0, 6.0)
    offsets = jnp.clip(1.5 * jax.random.normal(key_offset, (regions, H * HD), jnp.float32), -6.0, 6.0)
    total = noise + jnp.repeat(offsets, L_DEV, axis=0) + linked
    return jnp.clip(total, -12.0, 12.0).T.astype(jnp.bfloat16)


def levels(own_key, shape, pieces, least, top_value):
    loudness = 1.0
    for position, shards_of in pieces:
        draws = jax.random.uniform(jax.random.fold_in(jax.random.fold_in(own_key, 6), position), (shards_of,), jnp.float32, least / len(pieces), top_value / len(pieces))
        loudness = loudness * jnp.repeat(jnp.exp(draws), shape[position] // shards_of).reshape((-1,) + (1,) * (len(shape) - 1 - position))
    return loudness


def scatter_about(key, extent, spread, most, cuts=(), kind=jnp.bfloat16):
    entries = jax.random.normal(key, extent, jnp.float32) * spread
    if len(cuts) > 0:
        entries = levels(key, extent, cuts, -0.22, 0.18) * entries
    return jnp.clip(entries, min=-most, max=most).astype(kind)


def setup_inputs(seed: int = 0) -> dict:
    streams_of = jax.random.split(jax.random.key(seed), 7)
    queries = draw_queries(jax.random.fold_in(streams_of[6], 71), 0)
    keys = draw_keys(jax.random.fold_in(streams_of[6], 71), 0)
    values = draw_values(jax.random.fold_in(streams_of[6], 71), 0)
    feat_q = scatter_about(streams_of[3], (H, HD, HF), ((HD + 16) // 32) ** -0.5, 3.0, ((0, 8),))
    feat_k = scatter_about(streams_of[4], (H, HD, HF), ((HD + 16) // 32) ** -0.5, 3.0, ((0, 8),))
    mix = jnp.clip(jax.random.uniform(streams_of[5], (H,), jnp.float32, -2.0, 2.0) * levels(streams_of[5], (H,), ((0, 8),), -0.4, 0.0), -2.0, 2.0)
    return dict(queries=queries, keys=keys, values=values, feat_q=feat_q, feat_k=feat_k, mix=mix)


def feature_map(rows, weight):
    logits = jnp.einsum('rhd,hdf->hrf', rows.astype(jnp.float32), weight.astype(jnp.float32))
    halves = [jax.nn.softmax(logits, axis=-1), jax.nn.softmax(-logits, axis=-1)]
    return jnp.concatenate(halves, axis=-1).astype(jnp.bfloat16)

def attend_blocks(queries, phi_queries, keys_ext, values_ext, phi_keys, state, normer, gate, earlier):
    block = BLOCK
    count = queries.shape[0] // block
    head_dim = queries.shape[2]
    query_ids = jnp.arange(block)[:, None]
    window_ids = jnp.arange(block + WIN)[None, :]
    linear_ids = jnp.arange(block)[None, :]

    def advance(carry, index):
        states, norms = carry
        start = index * block
        query_rows = lax.dynamic_slice_in_dim(queries, start, block, 0).astype(jnp.float32)
        phi_rows = lax.dynamic_slice_in_dim(phi_queries, start, block, 1).astype(jnp.float32)
        window_keys = lax.dynamic_slice_in_dim(keys_ext, start, block + WIN, 0).astype(jnp.float32)
        window_values = lax.dynamic_slice_in_dim(values_ext, start, block + WIN, 0).astype(jnp.float32)
        phi_block = lax.dynamic_slice_in_dim(phi_keys, start, block, 1).astype(jnp.float32)
        value_block = lax.dynamic_slice_in_dim(values_ext, start, block, 0).astype(jnp.float32)
        keep = (window_ids > query_ids) & (window_ids <= query_ids + WIN)
        keep = keep & jnp.logical_or(start + window_ids >= WIN, earlier)
        scores = jnp.einsum('qhd,khd->hqk', query_rows, window_keys) / jnp.sqrt(jnp.float32(head_dim))
        scores = jnp.where(keep[None], scores, jnp.float32(-1e+30))
        top = lax.optimization_barrier(jnp.max(scores, axis=-1, keepdims=True))
        probs = jnp.exp(scores - top)
        total = lax.optimization_barrier(jnp.sum(probs, axis=-1))
        rounded = probs.astype(jnp.bfloat16).astype(jnp.float32)
        window = jnp.einsum('hqk,khd->qhd', rounded, window_values) / total.T[:, :, None]
        affinity = jnp.einsum('hqf,hkf->hqk', phi_rows, phi_block)
        affinity = jnp.where((linear_ids <= query_ids)[None], affinity, jnp.float32(0.0))
        affinity = affinity.astype(jnp.bfloat16).astype(jnp.float32)
        inner_num = jnp.einsum('hqk,khd->qhd', affinity, value_block)
        inner_den = lax.optimization_barrier(jnp.sum(affinity, axis=-1))
        cross_num = jnp.einsum('hqf,hfd->qhd', phi_rows, states, precision=lax.Precision.HIGHEST)
        cross_den = jnp.einsum('hqf,hf->hq', phi_rows, norms, precision=lax.Precision.HIGHEST)
        linear = (cross_num + inner_num) / (cross_den + inner_den + 1.0).T[:, :, None]
        mixed = gate[None, :, None] * window + (1.0 - gate)[None, :, None] * linear
        mixed = mixed.astype(jnp.bfloat16).reshape(block, -1)
        states = states + jnp.einsum('hkf,khd->hfd', phi_block, value_block)
        norms = norms + lax.optimization_barrier(jnp.sum(phi_block, axis=1))
        return ((states, norms), mixed)
    steps = jnp.arange(count, dtype=jnp.int32)
    _, outputs = lax.scan(advance, (state, normer), steps)
    return outputs.reshape(count * block, -1)

def reference(queries, keys, values, feat_q, feat_k, mix):
    query_rows = queries.T.reshape(TOKENS, H, HD)
    key_rows = keys.T.reshape(TOKENS, H, HD)
    value_rows = values.T.reshape(TOKENS, H, HD)
    padding = jnp.zeros((WIN, H, HD), jnp.bfloat16)
    keys_ext = jnp.concatenate([padding, key_rows], axis=0)
    values_ext = jnp.concatenate([padding, value_rows], axis=0)
    keep = (jnp.arange(TOKENS + WIN) >= WIN).astype(jnp.bfloat16)
    phi_queries = feature_map(query_rows, feat_q)
    phi_keys = feature_map(keys_ext, feat_k) * keep[None, :, None]
    state = jnp.zeros((H, 2 * HF, HD), jnp.float32)
    normer = jnp.zeros((H, 2 * HF), jnp.float32)
    gate = jax.nn.sigmoid(mix)
    return attend_blocks(query_rows, phi_queries, keys_ext, values_ext, phi_keys, state, normer, gate, jnp.asarray(False))
```

```python
import jax
import jax.numpy as jnp
from jax import lax
from jax.sharding import PartitionSpec as P

WIN = 64
BLOCK = 512
CHUNKS = 4


def passed_along(block, axis, distance):
    devices = range(lax.axis_size(axis))
    route = [(i - distance, i) for i in devices if i - distance in devices]
    return lax.ppermute(block, axis, route)


def exchange(rows, group, head_dim):
    moved = lax.all_to_all(rows, "seq", split_axis=1, concat_axis=0, tiled=True)
    return moved.reshape(group, head_dim, -1)


def feature_map(rows, weight):
    logits = jnp.einsum("hdt,hdf->htf", rows, weight, preferred_element_type=jnp.float32)
    halves = [jax.nn.softmax(logits, axis=-1), jax.nn.softmax(-logits, axis=-1)]
    return jnp.concatenate(halves, axis=-1).astype(jnp.bfloat16)


def window_chunk(q, k_cur, k_prev, v_cur, v_prev, first_masked):
    head_dim = q.shape[1]
    w = q.shape[3]
    scale = jnp.sqrt(jnp.float32(head_dim))
    s_cur = jnp.einsum("hdbt,hdbj->hbtj", q, k_cur, preferred_element_type=jnp.float32) / scale
    s_prev = jnp.einsum("hdbt,hdbj->hbtj", q, k_prev, preferred_element_type=jnp.float32) / scale
    ti = jnp.arange(w)[:, None]
    ji = jnp.arange(w)[None, :]
    keep_cur = ji <= ti
    keep_prev = ji > ti
    bi = jnp.arange(q.shape[2])[:, None, None]
    keep_prev = keep_prev[None] & jnp.logical_not((bi == 0) & first_masked)
    s_cur = jnp.where(keep_cur[None, None], s_cur, jnp.float32(-1e30))
    s_prev = jnp.where(keep_prev[None], s_prev, jnp.float32(-1e30))
    top = jnp.maximum(jnp.max(s_cur, axis=-1, keepdims=True), jnp.max(s_prev, axis=-1, keepdims=True))
    p_cur = jnp.exp(s_cur - top)
    p_prev = jnp.exp(s_prev - top)
    total = jnp.sum(p_cur, axis=-1) + jnp.sum(p_prev, axis=-1)
    out = jnp.einsum(
        "hbtj,hdbj->hbtd", p_cur.astype(jnp.bfloat16), v_cur, preferred_element_type=jnp.float32
    ) + jnp.einsum(
        "hbtj,hdbj->hbtd", p_prev.astype(jnp.bfloat16), v_prev, preferred_element_type=jnp.float32
    )
    return out / total[..., None]


def body(queries, keys, values, feat_q, feat_k, mix):
    shards = lax.axis_size("seq")
    place = lax.axis_index("seq")
    feature_rows = queries.shape[0]
    length = queries.shape[1] // shards
    group = feat_q.shape[0]
    head_dim = feat_q.shape[1]
    chunk = length // CHUNKS
    nb = chunk // WIN

    k = exchange(keys.reshape(feature_rows, shards, length), group, head_dim)
    v = exchange(values.reshape(feature_rows, shards, length), group, head_dim)
    qs = queries.reshape(feature_rows, shards, CHUNKS, chunk)
    q_parts = [exchange(qs[:, :, c, :], group, head_dim) for c in range(CHUNKS)]

    earlier = place > 0
    tails = jnp.stack([k[:, :, length - WIN :], v[:, :, length - WIN :]])
    before = passed_along(tails, "seq", 1)
    k_ext = jnp.concatenate([before[0], k], axis=2)
    v_ext = jnp.concatenate([before[1], v], axis=2)

    keep = jnp.logical_or(jnp.arange(length + WIN) >= WIN, earlier).astype(jnp.bfloat16)
    phi_k = feature_map(k_ext, feat_k) * keep[None, :, None]

    own_state = jnp.einsum(
        "htf,hdt->hfd", phi_k[:, WIN:], v, preferred_element_type=jnp.float32
    )
    own_norm = jnp.sum(phi_k[:, WIN:], axis=1, dtype=jnp.float32)
    gathered_state = lax.all_gather(own_state.astype(jnp.bfloat16), "seq")
    gathered_norm = lax.all_gather(own_norm.astype(jnp.bfloat16), "seq")
    below = (jnp.arange(shards) < place).astype(jnp.float32)
    prior_state = jnp.einsum(
        "s,shfd->hfd", below, gathered_state.astype(jnp.float32), precision=lax.Precision.HIGHEST
    )
    prior_norm = jnp.einsum(
        "s,shf->hf", below, gathered_norm.astype(jnp.float32), precision=lax.Precision.HIGHEST
    )

    halo_state = jnp.einsum(
        "htf,hdt->hfd", phi_k[:, :WIN], before[1], preferred_element_type=jnp.float32
    )
    halo_norm = jnp.sum(phi_k[:, :WIN], axis=1, dtype=jnp.float32)

    gate = jax.nn.sigmoid(mix)
    qi = jnp.arange(chunk)[:, None]
    ki = jnp.arange(chunk)[None, :]
    lin_keep = ki <= qi

    states = -halo_state
    norms = -halo_norm
    windows, nums, dens, phis = [], [], [], []
    for c in range(CHUNKS):
        start = c * chunk
        q = q_parts[c]
        phi_q = feature_map(q, feat_q)
        qb = q.reshape(group, head_dim, nb, WIN)
        k_cur = k[:, :, start : start + chunk].reshape(group, head_dim, nb, WIN)
        k_prev = k_ext[:, :, start : start + chunk].reshape(group, head_dim, nb, WIN)
        v_cur = v[:, :, start : start + chunk].reshape(group, head_dim, nb, WIN)
        v_prev = v_ext[:, :, start : start + chunk].reshape(group, head_dim, nb, WIN)
        first_masked = jnp.logical_and(c == 0, jnp.logical_not(earlier))
        win = window_chunk(qb, k_cur, k_prev, v_cur, v_prev, first_masked)
        windows.append(win.reshape(group, chunk, head_dim))

        phi_block = phi_k[:, start : start + chunk]
        value_block = v_ext[:, :, start : start + chunk]
        affinity = jnp.einsum("htf,hjf->htj", phi_q, phi_block, preferred_element_type=jnp.float32)
        affinity = jnp.where(lin_keep[None], affinity, jnp.float32(0.0)).astype(jnp.bfloat16)
        inner_num = jnp.einsum(
            "htj,hdj->htd", affinity, value_block, preferred_element_type=jnp.float32
        )
        inner_den = jnp.sum(affinity, axis=-1, dtype=jnp.float32)
        phi_wide = phi_q.astype(jnp.float32)
        cross_num = jnp.einsum("htf,hfd->htd", phi_wide, states, precision=lax.Precision.HIGHEST)
        cross_den = jnp.einsum("htf,hf->ht", phi_wide, norms, precision=lax.Precision.HIGHEST)
        nums.append(cross_num + inner_num)
        dens.append(cross_den + inner_den)
        phis.append(phi_q)
        if c + 1 < CHUNKS:
            states = states + jnp.einsum(
                "hjf,hdj->hfd", phi_block, value_block, preferred_element_type=jnp.float32
            )
            norms = norms + jnp.sum(phi_block, axis=1, dtype=jnp.float32)

    window = jnp.concatenate(windows, axis=1)
    num = jnp.concatenate(nums, axis=1)
    den = jnp.concatenate(dens, axis=1)
    phi_all = jnp.concatenate(phis, axis=1).astype(jnp.float32)
    prior_num = jnp.einsum("htf,hfd->htd", phi_all, prior_state, precision=lax.Precision.HIGHEST)
    prior_den = jnp.einsum("htf,hf->ht", phi_all, prior_norm, precision=lax.Precision.HIGHEST)
    linear = (num + prior_num) / (den + prior_den + 1.0)[..., None]
    mixed = gate[:, None, None] * window + (1.0 - gate)[:, None, None] * linear
    return mixed.astype(jnp.bfloat16).transpose(1, 0, 2).reshape(length, group * head_dim)


def solution(mesh):
    return jax.shard_map(
        body,
        mesh=mesh,
        in_specs=(
            P(("heads", "seq"), None),
            P(("heads", "seq"), None),
            P(("heads", "seq"), None),
            P("heads", None, None),
            P("heads", None, None),
            P("heads"),
        ),
        out_specs=P("seq", "heads"),
        check_vma=False,
    )
```

```python
import functools

import jax
import jax.numpy as jnp
from jax import lax
from jax.experimental import pallas as pl
from jax.experimental.pallas import tpu as pltpu
from jax.sharding import PartitionSpec as P

WIN = 64
QB = 128
INTERPRET = False


def passed_along(block, axis, distance):
    devices = range(lax.axis_size(axis))
    route = [(i - distance, i) for i in devices if i - distance in devices]
    return lax.ppermute(block, axis, route)


def exchange(rows, group, head_dim):
    moved = lax.all_to_all(rows, "seq", split_axis=1, concat_axis=0, tiled=True)
    return moved.reshape(group, head_dim, -1)


def feature_map(rows, weight):
    logits = jnp.einsum("hdt,hdf->htf", rows, weight, preferred_element_type=jnp.float32)
    halves = [jax.nn.softmax(logits, axis=-1), jax.nn.softmax(-logits, axis=-1)]
    return jnp.concatenate(halves, axis=-1).astype(jnp.bfloat16)


def _nt(a, b):
    return lax.dot_general(a, b, (((1,), (1,)), ((), ())), preferred_element_type=jnp.float32)


def attend_kernel(q_ref, k_ref, v_ref, pk_ref, fq_ref, st_ref, z_ref, g_ref, b_ref, o_ref):
    length = q_ref.shape[1]
    head_dim = q_ref.shape[2]
    feats = fq_ref.shape[2]
    half = feats // 2
    scale = jnp.sqrt(jnp.float32(head_dim))
    fq = fq_ref[0]
    g = g_ref[0]
    lane = lax.broadcasted_iota(jnp.int32, (QB, feats), 1)
    lo = lane < half
    tq = lax.broadcasted_iota(jnp.int32, (QB, 2 * QB), 0)
    wk = lax.broadcasted_iota(jnp.int32, (QB, 2 * QB), 1)
    win_keep = (wk > tq + WIN) & (wk <= tq + QB)
    lin_keep = wk <= tq + WIN
    neg = jnp.float32(-1e30)

    def step(i, carry):
        st, z = carry
        t0 = pl.multiple_of(i * QB, QB)
        q = q_ref[0, pl.ds(t0, QB), :]
        kw = k_ref[0, :, pl.ds(t0, 2 * QB)]
        vw = v_ref[0, :, pl.ds(t0, 2 * QB)]
        pkw = pk_ref[0, pl.ds(t0, 2 * QB), :]

        s = jnp.dot(q, kw, preferred_element_type=jnp.float32) / scale
        s = s + jnp.where(i == 0, b_ref[...], jnp.float32(0.0))
        s = jnp.where(win_keep, s, neg)
        top = jnp.max(s, axis=1, keepdims=True)
        p = jnp.exp(s - top)
        total = jnp.sum(p, axis=1, keepdims=True)
        window = _nt(p.astype(jnp.bfloat16), vw) / total

        logits = jnp.dot(q, fq, preferred_element_type=jnp.float32)
        m_lo = jnp.max(jnp.where(lo, logits, neg), axis=1, keepdims=True)
        m_hi = jnp.max(jnp.where(lo, neg, logits), axis=1, keepdims=True)
        e = jnp.exp(logits - jnp.where(lo, m_lo, m_hi))
        s_lo = jnp.sum(jnp.where(lo, e, 0.0), axis=1, keepdims=True)
        s_hi = jnp.sum(jnp.where(lo, 0.0, e), axis=1, keepdims=True)
        phi = (e / jnp.where(lo, s_lo, s_hi)).astype(jnp.bfloat16)

        aff = _nt(phi, pkw)
        aff = jnp.where(lin_keep, aff, jnp.float32(0.0)).astype(jnp.bfloat16)
        num = _nt(aff, vw)
        den = jnp.sum(aff.astype(jnp.float32), axis=1, keepdims=True)
        st_hi = st.astype(jnp.bfloat16)
        st_lo = (st - st_hi.astype(jnp.float32)).astype(jnp.bfloat16)
        num = num + _nt(phi, st_hi) + _nt(phi, st_lo)
        den = den + jnp.sum(phi.astype(jnp.float32) * z, axis=1, keepdims=True)
        linear = num / (den + 1.0)
        o_ref[pl.ds(t0, QB), :] = (g * window + (1.0 - g) * linear).astype(o_ref.dtype)

        vb = v_ref[0, :, pl.ds(t0, QB)]
        pkb = pk_ref[0, pl.ds(t0, QB), :]
        st = st + jnp.dot(vb, pkb, preferred_element_type=jnp.float32)
        z = z + jnp.sum(pkb.astype(jnp.float32), axis=0, keepdims=True)
        return st, z

    lax.fori_loop(0, length // QB, step, (st_ref[0], z_ref[0]))


def attend(q_tm, k_ext, v_ext, pk_ext, fq2, st0, z0, gate_rows, bias0):
    group, length, head_dim = q_tm.shape
    ext = k_ext.shape[2]
    feats = fq2.shape[2]
    return pl.pallas_call(
        attend_kernel,
        grid=(group,),
        in_specs=[
            pl.BlockSpec((1, length, head_dim), lambda h: (h, 0, 0)),
            pl.BlockSpec((1, head_dim, ext), lambda h: (h, 0, 0)),
            pl.BlockSpec((1, head_dim, ext), lambda h: (h, 0, 0)),
            pl.BlockSpec((1, ext, feats), lambda h: (h, 0, 0)),
            pl.BlockSpec((1, head_dim, feats), lambda h: (h, 0, 0)),
            pl.BlockSpec((1, head_dim, feats), lambda h: (h, 0, 0)),
            pl.BlockSpec((1, 1, feats), lambda h: (h, 0, 0)),
            pl.BlockSpec((1, 1, head_dim), lambda h: (h, 0, 0)),
            pl.BlockSpec((1, 2 * QB), lambda h: (0, 0)),
        ],
        out_specs=pl.BlockSpec((length, head_dim), lambda h: (0, h)),
        out_shape=jax.ShapeDtypeStruct((length, group * head_dim), jnp.bfloat16),
        interpret=INTERPRET,
    )(q_tm, k_ext, v_ext, pk_ext, fq2, st0, z0, gate_rows, bias0)


def local_part(q, k, v, before, earlier, feat_q, feat_k, prior_state, prior_norm, gate):
    group, head_dim, length = q.shape
    keep = earlier.astype(jnp.bfloat16)
    phi_k = feature_map(k, feat_k)
    phi_halo = feature_map(before[0], feat_k) * keep
    halo_state = jnp.einsum(
        "htf,hdt->hdf", phi_halo, before[1], preferred_element_type=jnp.float32
    )
    halo_norm = jnp.sum(phi_halo, axis=1, dtype=jnp.float32)
    feats = phi_k.shape[2]
    pad_k = jnp.zeros((group, head_dim, WIN), k.dtype)
    k_ext = jnp.concatenate([pad_k, before[0], k], axis=2)
    v_ext = jnp.concatenate([pad_k, before[1], v], axis=2)
    pk_ext = jnp.concatenate(
        [jnp.zeros((group, WIN, feats), phi_k.dtype), phi_halo, phi_k], axis=1
    )
    fq2 = jnp.concatenate([feat_q, -feat_q], axis=2)
    st0 = prior_state - halo_state
    z0 = (prior_norm - halo_norm)[:, None, :]
    gate_rows = jnp.broadcast_to(gate[:, None, None], (group, 1, head_dim)).astype(jnp.float32)
    halo_cols = (jnp.arange(2 * QB) >= WIN) & (jnp.arange(2 * QB) < 2 * WIN)
    bias0 = jnp.where(halo_cols & jnp.logical_not(earlier), jnp.float32(-1e30), jnp.float32(0.0))
    q_tm = q.transpose(0, 2, 1)
    return attend(q_tm, k_ext, v_ext, pk_ext, fq2, st0, z0, gate_rows, bias0[None, :])


def body(queries, keys, values, feat_q, feat_k, mix):
    shards = lax.axis_size("seq")
    place = lax.axis_index("seq")
    feature_rows = queries.shape[0]
    length = queries.shape[1] // shards
    group = feat_q.shape[0]
    head_dim = feat_q.shape[1]

    k = exchange(keys.reshape(feature_rows, shards, length), group, head_dim)
    v = exchange(values.reshape(feature_rows, shards, length), group, head_dim)
    q = exchange(queries.reshape(feature_rows, shards, length), group, head_dim)

    earlier = place > 0
    tails = jnp.stack([k[:, :, length - WIN :], v[:, :, length - WIN :]])
    before = passed_along(tails, "seq", 1)

    phi_own = feature_map(k, feat_k)
    own_state = jnp.einsum("htf,hdt->hdf", phi_own, v, preferred_element_type=jnp.float32)
    own_norm = jnp.sum(phi_own, axis=1, dtype=jnp.float32)
    gathered_state = lax.all_gather(own_state.astype(jnp.bfloat16), "seq")
    gathered_norm = lax.all_gather(own_norm.astype(jnp.bfloat16), "seq")
    below = (jnp.arange(shards) < place).astype(jnp.float32)
    prior_state = jnp.einsum(
        "s,shdf->hdf", below, gathered_state.astype(jnp.float32), precision=lax.Precision.HIGHEST
    )
    prior_norm = jnp.einsum(
        "s,shf->hf", below, gathered_norm.astype(jnp.float32), precision=lax.Precision.HIGHEST
    )
    gate = jax.nn.sigmoid(mix)
    return local_part(q, k, v, before, earlier, feat_q, feat_k, prior_state, prior_norm, gate)


def solution(mesh):
    return jax.shard_map(
        body,
        mesh=mesh,
        in_specs=(
            P(("heads", "seq"), None),
            P(("heads", "seq"), None),
            P(("heads", "seq"), None),
            P("heads", None, None),
            P("heads", None, None),
            P("heads"),
        ),
        out_specs=P("seq", "heads"),
        check_vma=False,
    )
```

```python
import functools

import jax
import jax.numpy as jnp
from jax import lax
from jax.experimental import pallas as pl
from jax.experimental.pallas import tpu as pltpu
from jax.sharding import PartitionSpec as P

WIN = 64
QB = 128
INTERPRET = False


def passed_along(block, axis, distance):
    devices = range(lax.axis_size(axis))
    route = [(i - distance, i) for i in devices if i - distance in devices]
    return lax.ppermute(block, axis, route)


def exchange(rows, group, head_dim):
    moved = lax.all_to_all(rows, "seq", split_axis=1, concat_axis=0, tiled=True)
    return moved.reshape(group, head_dim, -1)


def feature_map(rows, weight):
    logits = jnp.einsum("hdt,hdf->htf", rows, weight, preferred_element_type=jnp.float32)
    halves = [jax.nn.softmax(logits, axis=-1), jax.nn.softmax(-logits, axis=-1)]
    return jnp.concatenate(halves, axis=-1).astype(jnp.bfloat16)


def _nt(a, b):
    return lax.dot_general(a, b, (((1,), (1,)), ((), ())), preferred_element_type=jnp.float32)


def _tn(a, b):
    return lax.dot_general(a, b, (((0,), (0,)), ((), ())), preferred_element_type=jnp.float32)


def attend_kernel(
    q_ref, k_ref, v_ref, pk_ref, kh_ref, vh_ref, pkh_ref, fq_ref, st_ref, z_ref, g_ref, b_ref, o_ref
):
    length = q_ref.shape[2]
    head_dim = q_ref.shape[1]
    feats = fq_ref.shape[2]
    half = feats // 2
    inv_scale = 1.0 / jnp.sqrt(jnp.float32(head_dim))
    fq = fq_ref[0]
    g = g_ref[0]
    lane = lax.broadcasted_iota(jnp.int32, (QB, feats), 1)
    lo = lane < half
    tq = lax.broadcasted_iota(jnp.int32, (QB, 2 * QB), 0)
    wk = lax.broadcasted_iota(jnp.int32, (QB, 2 * QB), 1)
    win_keep = (wk > tq + WIN) & (wk <= tq + QB)
    lin_keep = wk <= tq + WIN
    neg = jnp.float32(-1e30)

    def step(t0, st, z, kw, vw, pkw, bias):
        q = q_ref[0, :, pl.ds(t0, QB)]
        s = _tn(q, kw) * inv_scale
        if bias is not None:
            s = s + bias
        s = jnp.where(win_keep, s, neg)
        top = jnp.max(s, axis=1, keepdims=True)
        p = jnp.exp(s - top)
        total = jnp.sum(p, axis=1, keepdims=True)
        window = _nt(p.astype(jnp.bfloat16), vw) * (1.0 / total)

        logits = _tn(q, fq)
        m_lo = jnp.max(jnp.where(lo, logits, neg), axis=1, keepdims=True)
        m_hi = jnp.max(jnp.where(lo, neg, logits), axis=1, keepdims=True)
        e = jnp.exp(logits - jnp.where(lo, m_lo, m_hi))
        s_lo = jnp.sum(jnp.where(lo, e, 0.0), axis=1, keepdims=True)
        s_hi = jnp.sum(jnp.where(lo, 0.0, e), axis=1, keepdims=True)
        phi = (e * jnp.where(lo, 1.0 / s_lo, 1.0 / s_hi)).astype(jnp.bfloat16)

        aff = _nt(phi, pkw)
        aff = jnp.where(lin_keep, aff, jnp.float32(0.0)).astype(jnp.bfloat16)
        num = _nt(aff, vw)
        den = jnp.sum(aff.astype(jnp.float32), axis=1, keepdims=True)
        st_hi = st.astype(jnp.bfloat16)
        st_lo = (st - st_hi.astype(jnp.float32)).astype(jnp.bfloat16)
        num = num + _nt(phi, st_hi) + _nt(phi, st_lo)
        den = den + jnp.sum(phi.astype(jnp.float32) * z, axis=1, keepdims=True)
        linear = num * (1.0 / (den + 1.0))
        o_ref[pl.ds(t0, QB), :] = (g * window + (1.0 - g) * linear).astype(o_ref.dtype)

        vb = vw[:, :QB]
        pkb = pkw[:QB]
        st = st + jnp.dot(vb, pkb, preferred_element_type=jnp.float32)
        z = z + jnp.sum(pkb.astype(jnp.float32), axis=0, keepdims=True)
        return st, z

    kw0 = jnp.concatenate([kh_ref[0], k_ref[0, :, pl.ds(0, QB)]], axis=1)
    vw0 = jnp.concatenate([vh_ref[0], v_ref[0, :, pl.ds(0, QB)]], axis=1)
    pkw0 = jnp.concatenate([pkh_ref[0], pk_ref[0, pl.ds(0, QB), :]], axis=0)
    carry = step(0, st_ref[0], z_ref[0], kw0, vw0, pkw0, b_ref[...])

    def loop(i, carry):
        t0 = pl.multiple_of(i * QB, QB)
        base = pl.multiple_of(t0 - QB, QB)
        kw = k_ref[0, :, pl.ds(base, 2 * QB)]
        vw = v_ref[0, :, pl.ds(base, 2 * QB)]
        pkw = pk_ref[0, pl.ds(base, 2 * QB), :]
        return step(t0, carry[0], carry[1], kw, vw, pkw, None)

    lax.fori_loop(1, length // QB, loop, carry)


def attend(q, k, v, pk, kh, vh, pkh, fq2, st0, z0, gate_rows, bias0):
    group, head_dim, length = q.shape
    feats = fq2.shape[2]
    return pl.pallas_call(
        attend_kernel,
        grid=(group,),
        in_specs=[
            pl.BlockSpec((1, head_dim, length), lambda h: (h, 0, 0)),
            pl.BlockSpec((1, head_dim, length), lambda h: (h, 0, 0)),
            pl.BlockSpec((1, head_dim, length), lambda h: (h, 0, 0)),
            pl.BlockSpec((1, length, feats), lambda h: (h, 0, 0)),
            pl.BlockSpec((1, head_dim, QB), lambda h: (h, 0, 0)),
            pl.BlockSpec((1, head_dim, QB), lambda h: (h, 0, 0)),
            pl.BlockSpec((1, QB, feats), lambda h: (h, 0, 0)),
            pl.BlockSpec((1, head_dim, feats), lambda h: (h, 0, 0)),
            pl.BlockSpec((1, head_dim, feats), lambda h: (h, 0, 0)),
            pl.BlockSpec((1, 1, feats), lambda h: (h, 0, 0)),
            pl.BlockSpec((1, 1, head_dim), lambda h: (h, 0, 0)),
            pl.BlockSpec((1, 2 * QB), lambda h: (0, 0)),
        ],
        out_specs=pl.BlockSpec((length, head_dim), lambda h: (0, h)),
        out_shape=jax.ShapeDtypeStruct((length, group * head_dim), jnp.bfloat16),
        interpret=INTERPRET,
    )(q, k, v, pk, kh, vh, pkh, fq2, st0, z0, gate_rows, bias0)


def local_part(q, k, v, before, earlier, feat_q, feat_k, prior_state, prior_norm, gate):
    group, head_dim, length = q.shape
    keep = earlier.astype(jnp.bfloat16)
    phi_k = feature_map(k, feat_k)
    phi_halo = feature_map(before[0], feat_k) * keep
    halo_state = jnp.einsum(
        "htf,hdt->hdf", phi_halo, before[1], preferred_element_type=jnp.float32
    )
    halo_norm = jnp.sum(phi_halo, axis=1, dtype=jnp.float32)
    feats = phi_k.shape[2]
    pad_k = jnp.zeros((group, head_dim, QB - WIN), k.dtype)
    kh = jnp.concatenate([pad_k, before[0]], axis=2)
    vh = jnp.concatenate([pad_k, before[1]], axis=2)
    pkh = jnp.concatenate([jnp.zeros((group, QB - WIN, feats), phi_k.dtype), phi_halo], axis=1)
    fq2 = jnp.concatenate([feat_q, -feat_q], axis=2)
    st0 = prior_state - halo_state
    z0 = (prior_norm - halo_norm)[:, None, :]
    gate_rows = jnp.broadcast_to(gate[:, None, None], (group, 1, head_dim)).astype(jnp.float32)
    halo_cols = (jnp.arange(2 * QB) >= QB - WIN) & (jnp.arange(2 * QB) < QB)
    bias0 = jnp.where(halo_cols & jnp.logical_not(earlier), jnp.float32(-1e30), jnp.float32(0.0))
    return attend(q, k, v, phi_k, kh, vh, pkh, fq2, st0, z0, gate_rows, bias0[None, :])


def body(queries, keys, values, feat_q, feat_k, mix):
    shards = lax.axis_size("seq")
    place = lax.axis_index("seq")
    feature_rows = queries.shape[0]
    length = queries.shape[1] // shards
    group = feat_q.shape[0]
    head_dim = feat_q.shape[1]

    k = exchange(keys.reshape(feature_rows, shards, length), group, head_dim)
    v = exchange(values.reshape(feature_rows, shards, length), group, head_dim)
    q = exchange(queries.reshape(feature_rows, shards, length), group, head_dim)

    earlier = place > 0
    tails = jnp.stack([k[:, :, length - WIN :], v[:, :, length - WIN :]])
    before = passed_along(tails, "seq", 1)

    phi_own = feature_map(k, feat_k)
    own_state = jnp.einsum("htf,hdt->hdf", phi_own, v, preferred_element_type=jnp.float32)
    own_norm = jnp.sum(phi_own, axis=1, dtype=jnp.float32)
    own = jnp.concatenate(
        [own_state.reshape(group * head_dim, -1), own_norm], axis=0
    ).astype(jnp.bfloat16)
    gathered = lax.all_gather(own, "seq").astype(jnp.float32)
    below = (jnp.arange(shards) < place).astype(jnp.float32)
    prior = jnp.einsum("s,srf->rf", below, gathered, precision=lax.Precision.HIGHEST)
    prior_state = prior[: group * head_dim].reshape(own_state.shape)
    prior_norm = prior[group * head_dim :]
    gate = jax.nn.sigmoid(mix)
    return local_part(q, k, v, before, earlier, feat_q, feat_k, prior_state, prior_norm, gate)


def solution(mesh):
    return jax.shard_map(
        body,
        mesh=mesh,
        in_specs=(
            P(("heads", "seq"), None),
            P(("heads", "seq"), None),
            P(("heads", "seq"), None),
            P("heads", None, None),
            P("heads", None, None),
            P("heads"),
        ),
        out_specs=P("seq", "heads"),
        check_vma=False,
    )
```

```python
import functools

import jax
import jax.numpy as jnp
from jax import lax
from jax.experimental import pallas as pl
from jax.experimental.pallas import tpu as pltpu
from jax.sharding import PartitionSpec as P

WIN = 64
QB = 128
HEADS_PER_STEP = 2
INTERPRET = False


def passed_along(block, axis, distance):
    devices = range(lax.axis_size(axis))
    route = [(i - distance, i) for i in devices if i - distance in devices]
    return lax.ppermute(block, axis, route)


def exchange(rows, group, head_dim):
    moved = lax.all_to_all(rows, "seq", split_axis=1, concat_axis=0, tiled=True)
    return moved.reshape(group, head_dim, -1)


def feature_map(rows, weight):
    logits = jnp.einsum("hdt,hdf->htf", rows, weight, preferred_element_type=jnp.float32)
    halves = [jax.nn.softmax(logits, axis=-1), jax.nn.softmax(-logits, axis=-1)]
    return jnp.concatenate(halves, axis=-1).astype(jnp.bfloat16)


def _nt(a, b):
    return lax.dot_general(a, b, (((1,), (1,)), ((), ())), preferred_element_type=jnp.float32)


def _tn(a, b):
    return lax.dot_general(a, b, (((0,), (0,)), ((), ())), preferred_element_type=jnp.float32)


def attend_kernel(
    q_ref, k_ref, v_ref, pk_ref, kh_ref, vh_ref, pkh_ref, fq_ref, st_ref, z_ref, g_ref, b_ref, o_ref
):
    heads = q_ref.shape[0]
    length = q_ref.shape[2]
    head_dim = q_ref.shape[1]
    feats = fq_ref.shape[1]
    half = feats // 2
    inv_scale = 1.0 / jnp.sqrt(jnp.float32(head_dim))
    row = lax.broadcasted_iota(jnp.int32, (feats, QB), 0)
    lo = row < half
    wk = lax.broadcasted_iota(jnp.int32, (2 * QB, QB), 0)
    tq = lax.broadcasted_iota(jnp.int32, (2 * QB, QB), 1)
    win_keep = (wk > tq + WIN) & (wk <= tq + QB)
    lin_keep = wk <= tq + WIN
    zrow = lax.broadcasted_iota(jnp.int32, (8, feats), 0)
    neg = jnp.float32(-1e30)

    def step(hh, t0, st, z, kw, vw, pkw, bias):
        q = q_ref[hh, :, pl.ds(t0, QB)]
        g = g_ref[hh]
        s = jnp.dot(kw, q, preferred_element_type=jnp.float32) * inv_scale
        if bias is not None:
            s = s + bias
        s = jnp.where(win_keep, s, neg)
        top = jnp.max(s, axis=0, keepdims=True)
        p = jnp.exp(s - top)
        total = jnp.sum(p, axis=0, keepdims=True)
        window = jnp.dot(vw, p.astype(jnp.bfloat16), preferred_element_type=jnp.float32) * (1.0 / total)

        logits = jnp.dot(fq_ref[hh], q, preferred_element_type=jnp.float32)
        m_lo = jnp.max(logits[:half], axis=0, keepdims=True)
        m_hi = jnp.max(logits[half:], axis=0, keepdims=True)
        e = jnp.exp(logits - jnp.where(lo, m_lo, m_hi))
        s_lo = jnp.sum(e[:half], axis=0, keepdims=True)
        s_hi = jnp.sum(e[half:], axis=0, keepdims=True)
        phi = (e * jnp.where(lo, 1.0 / s_lo, 1.0 / s_hi)).astype(jnp.bfloat16)

        aff = jnp.dot(pkw, phi, preferred_element_type=jnp.float32)
        aff = jnp.where(lin_keep, aff, jnp.float32(0.0)).astype(jnp.bfloat16)
        num = jnp.dot(vw, aff, preferred_element_type=jnp.float32)
        den = jnp.sum(aff.astype(jnp.float32), axis=0, keepdims=True)
        st_hi = st.astype(jnp.bfloat16)
        st_lo = (st - st_hi.astype(jnp.float32)).astype(jnp.bfloat16)
        num = num + jnp.dot(st_hi, phi, preferred_element_type=jnp.float32)
        num = num + jnp.dot(st_lo, phi, preferred_element_type=jnp.float32)
        z_hi = z.astype(jnp.bfloat16)
        z_lo = (z - z_hi.astype(jnp.float32)).astype(jnp.bfloat16)
        zz = jnp.where(zrow == 0, z_hi, jnp.where(zrow == 1, z_lo, jnp.zeros_like(z_lo)))
        cross = jnp.dot(zz, phi, preferred_element_type=jnp.float32)
        den = den + (cross[0:1] + cross[1:2])
        linear = num * (1.0 / (den + 1.0))
        out = g * window + (1.0 - g) * linear
        o_ref[pl.ds(t0, QB), pl.ds(hh * head_dim, head_dim)] = out.T.astype(o_ref.dtype)

        vb = vw[:, :QB]
        pkb = pkw[:QB]
        st = st + jnp.dot(vb, pkb, preferred_element_type=jnp.float32)
        z = z + jnp.sum(pkb.astype(jnp.float32), axis=0, keepdims=True)
        return st, z

    carry = []
    for hh in range(heads):
        kw0 = jnp.concatenate([kh_ref[hh], k_ref[hh, pl.ds(0, QB), :]], axis=0)
        vw0 = jnp.concatenate([vh_ref[hh], v_ref[hh, :, pl.ds(0, QB)]], axis=1)
        pkw0 = jnp.concatenate([pkh_ref[hh], pk_ref[hh, pl.ds(0, QB), :]], axis=0)
        carry.append(step(hh, 0, st_ref[hh], z_ref[hh][0:1], kw0, vw0, pkw0, b_ref[...]))

    def loop(i, carry):
        t0 = pl.multiple_of(i * QB, QB)
        base = pl.multiple_of(t0 - QB, QB)
        out = []
        for hh in range(heads):
            kw = k_ref[hh, pl.ds(base, 2 * QB), :]
            vw = v_ref[hh, :, pl.ds(base, 2 * QB)]
            pkw = pk_ref[hh, pl.ds(base, 2 * QB), :]
            out.append(step(hh, t0, carry[hh][0], carry[hh][1], kw, vw, pkw, None))
        return tuple(out)

    lax.fori_loop(1, length // QB, loop, tuple(carry))


def attend(q, k_tm, v, pk, kh, vh, pkh, fq_t, st0, z0, gate_rows, bias0):
    group, head_dim, length = q.shape
    feats = fq_t.shape[1]
    hb = HEADS_PER_STEP
    return pl.pallas_call(
        attend_kernel,
        grid=(group // hb,),
        in_specs=[
            pl.BlockSpec((hb, head_dim, length), lambda h: (h, 0, 0)),
            pl.BlockSpec((hb, length, head_dim), lambda h: (h, 0, 0)),
            pl.BlockSpec((hb, head_dim, length), lambda h: (h, 0, 0)),
            pl.BlockSpec((hb, length, feats), lambda h: (h, 0, 0)),
            pl.BlockSpec((hb, QB, head_dim), lambda h: (h, 0, 0)),
            pl.BlockSpec((hb, head_dim, QB), lambda h: (h, 0, 0)),
            pl.BlockSpec((hb, QB, feats), lambda h: (h, 0, 0)),
            pl.BlockSpec((hb, feats, head_dim), lambda h: (h, 0, 0)),
            pl.BlockSpec((hb, head_dim, feats), lambda h: (h, 0, 0)),
            pl.BlockSpec((hb, 8, feats), lambda h: (h, 0, 0)),
            pl.BlockSpec((hb, 1, QB), lambda h: (h, 0, 0)),
            pl.BlockSpec((2 * QB, QB), lambda h: (0, 0)),
        ],
        out_specs=pl.BlockSpec((length, hb * head_dim), lambda h: (0, h)),
        out_shape=jax.ShapeDtypeStruct((length, group * head_dim), jnp.bfloat16),
        interpret=INTERPRET,
    )(q, k_tm, v, pk, kh, vh, pkh, fq_t, st0, z0, gate_rows, bias0)


def local_part(q, k, v, before, earlier, feat_q, feat_k, prior_state, prior_norm, gate):
    group, head_dim, length = q.shape
    keep = earlier.astype(jnp.bfloat16)
    phi_k = feature_map(k, feat_k)
    phi_halo = feature_map(before[0], feat_k) * keep
    halo_state = jnp.einsum(
        "htf,hdt->hdf", phi_halo, before[1], preferred_element_type=jnp.float32
    )
    halo_norm = jnp.sum(phi_halo, axis=1, dtype=jnp.float32)
    feats = phi_k.shape[2]
    pad_k = jnp.zeros((group, head_dim, QB - WIN), k.dtype)
    kh = jnp.concatenate([pad_k, before[0]], axis=2).transpose(0, 2, 1)
    vh = jnp.concatenate([pad_k, before[1]], axis=2)
    pkh = jnp.concatenate([jnp.zeros((group, QB - WIN, feats), phi_k.dtype), phi_halo], axis=1)
    fq_t = jnp.concatenate([feat_q, -feat_q], axis=2).transpose(0, 2, 1)
    st0 = prior_state - halo_state
    z0 = jnp.pad((prior_norm - halo_norm)[:, None, :], ((0, 0), (0, 7), (0, 0)))
    gate_rows = jnp.broadcast_to(gate[:, None, None], (group, 1, QB)).astype(jnp.float32)
    halo_rows = (jnp.arange(2 * QB) >= QB - WIN) & (jnp.arange(2 * QB) < QB)
    bias0 = jnp.where(halo_rows & jnp.logical_not(earlier), jnp.float32(-1e30), jnp.float32(0.0))
    bias0 = jnp.broadcast_to(bias0[:, None], (2 * QB, QB))
    k_tm = k.transpose(0, 2, 1)
    return attend(q, k_tm, v, phi_k, kh, vh, pkh, fq_t, st0, z0, gate_rows, bias0)


def body(queries, keys, values, feat_q, feat_k, mix):
    shards = lax.axis_size("seq")
    place = lax.axis_index("seq")
    feature_rows = queries.shape[0]
    length = queries.shape[1] // shards
    group = feat_q.shape[0]
    head_dim = feat_q.shape[1]

    k = exchange(keys.reshape(feature_rows, shards, length), group, head_dim)
    v = exchange(values.reshape(feature_rows, shards, length), group, head_dim)
    q = exchange(queries.reshape(feature_rows, shards, length), group, head_dim)

    earlier = place > 0
    tails = jnp.stack([k[:, :, length - WIN :], v[:, :, length - WIN :]])
    before = passed_along(tails, "seq", 1)

    phi_own = feature_map(k, feat_k)
    own_state = jnp.einsum("htf,hdt->hdf", phi_own, v, preferred_element_type=jnp.float32)
    own_norm = jnp.sum(phi_own, axis=1, dtype=jnp.float32)
    own = jnp.concatenate(
        [own_state.reshape(group * head_dim, -1), own_norm], axis=0
    ).astype(jnp.bfloat16)
    gathered = lax.all_gather(own, "seq").astype(jnp.float32)
    below = (jnp.arange(shards) < place).astype(jnp.float32)
    prior = jnp.einsum("s,srf->rf", below, gathered, precision=lax.Precision.HIGHEST)
    prior_state = prior[: group * head_dim].reshape(own_state.shape)
    prior_norm = prior[group * head_dim :]
    gate = jax.nn.sigmoid(mix)
    return local_part(q, k, v, before, earlier, feat_q, feat_k, prior_state, prior_norm, gate)


def solution(mesh):
    return jax.shard_map(
        body,
        mesh=mesh,
        in_specs=(
            P(("heads", "seq"), None),
            P(("heads", "seq"), None),
            P(("heads", "seq"), None),
            P("heads", None, None),
            P("heads", None, None),
            P("heads"),
        ),
        out_specs=P("seq", "heads"),
        check_vma=False,
    )
```

```python
import functools

import jax
import jax.numpy as jnp
from jax import lax
from jax.experimental import pallas as pl
from jax.experimental.pallas import tpu as pltpu
from jax.sharding import PartitionSpec as P

WIN = 64
QB = 128
HEADS_PER_STEP = 2
Q_PIECES = 2
INTERPRET = False


def passed_along(block, axis, distance):
    devices = range(lax.axis_size(axis))
    route = [(i - distance, i) for i in devices if i - distance in devices]
    return lax.ppermute(block, axis, route)


def exchange(rows, group, head_dim):
    moved = lax.all_to_all(rows, "seq", split_axis=1, concat_axis=0, tiled=True)
    return moved.reshape(group, head_dim, -1)


def feature_map(rows, weight):
    logits = jnp.einsum("hdt,hdf->htf", rows, weight, preferred_element_type=jnp.float32)
    halves = [jax.nn.softmax(logits, axis=-1), jax.nn.softmax(-logits, axis=-1)]
    return jnp.concatenate(halves, axis=-1).astype(jnp.bfloat16)


def _nt(a, b):
    return lax.dot_general(a, b, (((1,), (1,)), ((), ())), preferred_element_type=jnp.float32)


def _tn(a, b):
    return lax.dot_general(a, b, (((0,), (0,)), ((), ())), preferred_element_type=jnp.float32)


def make_kernel(t_begin, blocks):
    first = t_begin == 0

    def attend_kernel(*refs):
        (q_ref, k_ref, v_ref, pk_ref, kh_ref, vh_ref, pkh_ref, fq_ref, st_ref, z_ref, g_ref, b_ref) = refs[:12]
        if first:
            o_ref, st_out, z_out = refs[12:]
        else:
            o_ref = refs[13]
        heads = q_ref.shape[0]
        head_dim = q_ref.shape[1]
        feats = fq_ref.shape[1]
        half = feats // 2
        inv_scale = 1.0 / jnp.sqrt(jnp.float32(head_dim))
        row = lax.broadcasted_iota(jnp.int32, (feats, QB), 0)
        lo = row < half
        wk = lax.broadcasted_iota(jnp.int32, (2 * QB, QB), 0)
        tq = lax.broadcasted_iota(jnp.int32, (2 * QB, QB), 1)
        win_keep = (wk > tq + WIN) & (wk <= tq + QB)
        lin_keep = wk <= tq + WIN
        zrow = lax.broadcasted_iota(jnp.int32, (8, feats), 0)
        neg = jnp.float32(-1e30)

        def step(hh, t0, st, z, kw, vw, pkw, bias):
            q = q_ref[hh, :, pl.ds(t0 - t_begin, QB)]
            g = g_ref[hh]
            s = jnp.dot(kw, q, preferred_element_type=jnp.float32) * inv_scale
            if bias is not None:
                s = s + bias
            s = jnp.where(win_keep, s, neg)
            top = jnp.max(s, axis=0, keepdims=True)
            p = jnp.exp(s - top)
            total = jnp.sum(p, axis=0, keepdims=True)
            window = jnp.dot(vw, p.astype(jnp.bfloat16), preferred_element_type=jnp.float32)
            window = window * (1.0 / total)

            logits = jnp.dot(fq_ref[hh], q, preferred_element_type=jnp.float32)
            m_lo = jnp.max(logits[:half], axis=0, keepdims=True)
            m_hi = jnp.max(logits[half:], axis=0, keepdims=True)
            e = jnp.exp(logits - jnp.where(lo, m_lo, m_hi))
            s_lo = jnp.sum(e[:half], axis=0, keepdims=True)
            s_hi = jnp.sum(e[half:], axis=0, keepdims=True)
            phi = (e * jnp.where(lo, 1.0 / s_lo, 1.0 / s_hi)).astype(jnp.bfloat16)

            aff = jnp.dot(pkw, phi, preferred_element_type=jnp.float32)
            aff = jnp.where(lin_keep, aff, jnp.float32(0.0)).astype(jnp.bfloat16)
            num = jnp.dot(vw, aff, preferred_element_type=jnp.float32)
            den = jnp.sum(aff.astype(jnp.float32), axis=0, keepdims=True)
            st_hi = st.astype(jnp.bfloat16)
            st_lo = (st - st_hi.astype(jnp.float32)).astype(jnp.bfloat16)
            num = num + jnp.dot(st_hi, phi, preferred_element_type=jnp.float32)
            num = num + jnp.dot(st_lo, phi, preferred_element_type=jnp.float32)
            z_hi = z.astype(jnp.bfloat16)
            z_lo = (z - z_hi.astype(jnp.float32)).astype(jnp.bfloat16)
            zz = jnp.where(zrow == 0, z_hi, jnp.where(zrow == 1, z_lo, jnp.zeros_like(z_lo)))
            cross = jnp.dot(zz, phi, preferred_element_type=jnp.float32)
            den = den + (cross[0:1] + cross[1:2])
            linear = num * (1.0 / (den + 1.0))
            out = g * window + (1.0 - g) * linear
            rows = pl.ds(t0 - t_begin, QB)
            o_ref[rows, pl.ds(hh * head_dim, head_dim)] = out.T.astype(o_ref.dtype)

            vb = vw[:, :QB]
            pkb = pkw[:QB]
            st = st + jnp.dot(vb, pkb, preferred_element_type=jnp.float32)
            z = z + jnp.sum(pkb.astype(jnp.float32), axis=0, keepdims=True)
            return st, z

        carry = []
        for hh in range(heads):
            if first:
                kw0 = jnp.concatenate([kh_ref[hh], k_ref[hh, pl.ds(0, QB), :]], axis=0)
                vw0 = jnp.concatenate([vh_ref[hh], v_ref[hh, :, pl.ds(0, QB)]], axis=1)
                pkw0 = jnp.concatenate([pkh_ref[hh], pk_ref[hh, pl.ds(0, QB), :]], axis=0)
                carry.append(step(hh, 0, st_ref[hh], z_ref[hh][0:1], kw0, vw0, pkw0, b_ref[...]))
            else:
                carry.append((st_ref[hh], z_ref[hh][0:1]))

        def loop(i, carry):
            t0 = pl.multiple_of(i * QB, QB)
            base = pl.multiple_of(t0 - QB, QB)
            out = []
            for hh in range(heads):
                kw = k_ref[hh, pl.ds(base, 2 * QB), :]
                vw = v_ref[hh, :, pl.ds(base, 2 * QB)]
                pkw = pk_ref[hh, pl.ds(base, 2 * QB), :]
                out.append(step(hh, t0, carry[hh][0], carry[hh][1], kw, vw, pkw, None))
            return tuple(out)

        lo_blk = t_begin // QB + (1 if first else 0)
        final = lax.fori_loop(lo_blk, t_begin // QB + blocks, loop, tuple(carry))
        if first:
            for hh in range(heads):
                st_out[hh] = final[hh][0]
                z_out[hh] = jnp.broadcast_to(final[hh][1], (8, feats))

    return attend_kernel


def attend(q, t_begin, k_tm, v, pk, kh, vh, pkh, fq_t, st0, z0, gate_rows, bias0, prev):
    group, head_dim, span = q.shape
    length = v.shape[2]
    feats = fq_t.shape[1]
    hb = HEADS_PER_STEP
    first = prev is None
    in_specs = [
        pl.BlockSpec((hb, head_dim, span), lambda h: (h, 0, 0)),
        pl.BlockSpec((hb, length, head_dim), lambda h: (h, 0, 0)),
        pl.BlockSpec((hb, head_dim, length), lambda h: (h, 0, 0)),
        pl.BlockSpec((hb, length, feats), lambda h: (h, 0, 0)),
        pl.BlockSpec((hb, QB, head_dim), lambda h: (h, 0, 0)),
        pl.BlockSpec((hb, head_dim, QB), lambda h: (h, 0, 0)),
        pl.BlockSpec((hb, QB, feats), lambda h: (h, 0, 0)),
        pl.BlockSpec((hb, feats, head_dim), lambda h: (h, 0, 0)),
        pl.BlockSpec((hb, head_dim, feats), lambda h: (h, 0, 0)),
        pl.BlockSpec((hb, 8, feats), lambda h: (h, 0, 0)),
        pl.BlockSpec((hb, 1, QB), lambda h: (h, 0, 0)),
        pl.BlockSpec((2 * QB, QB), lambda h: (0, 0)),
    ]
    args = [q, k_tm, v, pk, kh, vh, pkh, fq_t, st0, z0, gate_rows, bias0]
    piece = t_begin // span
    out_spec = pl.BlockSpec((span, hb * head_dim), lambda h: (piece, h))
    out_shape = jax.ShapeDtypeStruct((length, group * head_dim), jnp.bfloat16)
    if first:
        out_specs = [
            out_spec,
            pl.BlockSpec((hb, head_dim, feats), lambda h: (h, 0, 0)),
            pl.BlockSpec((hb, 8, feats), lambda h: (h, 0, 0)),
        ]
        out_shapes = [
            out_shape,
            jax.ShapeDtypeStruct(st0.shape, jnp.float32),
            jax.ShapeDtypeStruct(z0.shape, jnp.float32),
        ]
        aliases = {}
    else:
        in_specs.append(pl.BlockSpec(memory_space=pl.ANY))
        args.append(prev)
        out_specs = out_spec
        out_shapes = out_shape
        aliases = {12: 0}
    return pl.pallas_call(
        make_kernel(t_begin, span // QB),
        grid=(group // hb,),
        in_specs=in_specs,
        out_specs=out_specs,
        out_shape=out_shapes,
        input_output_aliases=aliases,
        interpret=INTERPRET,
    )(*args)


def local_part(q_parts, k, v, before, earlier, feat_q, feat_k, prior_state, prior_norm, gate):
    group, head_dim, length = k.shape
    keep = earlier.astype(jnp.bfloat16)
    phi_k = feature_map(k, feat_k)
    phi_halo = feature_map(before[0], feat_k) * keep
    halo_state = jnp.einsum(
        "htf,hdt->hdf", phi_halo, before[1], preferred_element_type=jnp.float32
    )
    halo_norm = jnp.sum(phi_halo, axis=1, dtype=jnp.float32)
    feats = phi_k.shape[2]
    pad_k = jnp.zeros((group, head_dim, QB - WIN), k.dtype)
    kh = jnp.concatenate([pad_k, before[0]], axis=2).transpose(0, 2, 1)
    vh = jnp.concatenate([pad_k, before[1]], axis=2)
    pkh = jnp.concatenate([jnp.zeros((group, QB - WIN, feats), phi_k.dtype), phi_halo], axis=1)
    fq_t = jnp.concatenate([feat_q, -feat_q], axis=2).transpose(0, 2, 1)
    st = prior_state - halo_state
    z = jnp.pad((prior_norm - halo_norm)[:, None, :], ((0, 0), (0, 7), (0, 0)))
    gate_rows = jnp.broadcast_to(gate[:, None, None], (group, 1, QB)).astype(jnp.float32)
    halo_rows = (jnp.arange(2 * QB) >= QB - WIN) & (jnp.arange(2 * QB) < QB)
    bias0 = jnp.where(halo_rows & jnp.logical_not(earlier), jnp.float32(-1e30), jnp.float32(0.0))
    bias0 = jnp.broadcast_to(bias0[:, None], (2 * QB, QB))
    k_tm = k.transpose(0, 2, 1)
    span = q_parts[0].shape[2]
    out, st, z = attend(q_parts[0], 0, k_tm, v, phi_k, kh, vh, pkh, fq_t, st, z, gate_rows, bias0, None)
    for c in range(1, len(q_parts)):
        out = attend(q_parts[c], c * span, k_tm, v, phi_k, kh, vh, pkh, fq_t, st, z, gate_rows, bias0, out)
    return out


def body(queries, keys, values, feat_q, feat_k, mix):
    shards = lax.axis_size("seq")
    place = lax.axis_index("seq")
    feature_rows = queries.shape[0]
    length = queries.shape[1] // shards
    group = feat_q.shape[0]
    head_dim = feat_q.shape[1]

    k = exchange(keys.reshape(feature_rows, shards, length), group, head_dim)
    v = exchange(values.reshape(feature_rows, shards, length), group, head_dim)
    halves = queries.reshape(feature_rows, shards, Q_PIECES, length // Q_PIECES).transpose(2, 1, 0, 3)
    q_parts = [
        lax.all_to_all(halves[c], "seq", split_axis=0, concat_axis=0, tiled=True).reshape(
            group, head_dim, -1
        )
        for c in range(Q_PIECES)
    ]

    earlier = place > 0
    tails = jnp.stack([k[:, :, length - WIN :], v[:, :, length - WIN :]])
    before = passed_along(tails, "seq", 1)

    phi_own = feature_map(k, feat_k)
    own_state = jnp.einsum("htf,hdt->hdf", phi_own, v, preferred_element_type=jnp.float32)
    own_norm = jnp.sum(phi_own, axis=1, dtype=jnp.float32)
    own = jnp.concatenate(
        [own_state.reshape(group * head_dim, -1), own_norm], axis=0
    ).astype(jnp.bfloat16)
    gathered = lax.all_gather(own, "seq").astype(jnp.float32)
    below = (jnp.arange(shards) < place).astype(jnp.float32)
    prior = jnp.einsum("s,srf->rf", below, gathered, precision=lax.Precision.HIGHEST)
    prior_state = prior[: group * head_dim].reshape(own_state.shape)
    prior_norm = prior[group * head_dim :]
    gate = jax.nn.sigmoid(mix)
    return local_part(q_parts, k, v, before, earlier, feat_q, feat_k, prior_state, prior_norm, gate)


def solution(mesh):
    return jax.shard_map(
        body,
        mesh=mesh,
        in_specs=(
            P(("heads", "seq"), None),
            P(("heads", "seq"), None),
            P(("heads", "seq"), None),
            P("heads", None, None),
            P("heads", None, None),
            P("heads"),
        ),
        out_specs=P("seq", "heads"),
        check_vma=False,
    )
```

```python
import functools

import jax
import jax.numpy as jnp
from jax import lax
from jax.experimental import pallas as pl
from jax.experimental.pallas import tpu as pltpu
from jax.sharding import PartitionSpec as P

WIN = 64
QB = 128
HEADS_PER_STEP = 2
Q_PIECES = 2
INTERPRET = False


def passed_along(block, axis, distance):
    devices = range(lax.axis_size(axis))
    route = [(i - distance, i) for i in devices if i - distance in devices]
    return lax.ppermute(block, axis, route)


def exchange(rows, group, head_dim):
    moved = lax.all_to_all(rows, "seq", split_axis=1, concat_axis=0, tiled=True)
    return moved.reshape(group, head_dim, -1)


def feature_map(rows, weight):
    logits = jnp.einsum("hdt,hdf->htf", rows, weight, preferred_element_type=jnp.float32)
    halves = [jax.nn.softmax(logits, axis=-1), jax.nn.softmax(-logits, axis=-1)]
    return jnp.concatenate(halves, axis=-1).astype(jnp.bfloat16)


def _nt(a, b):
    return lax.dot_general(a, b, (((1,), (1,)), ((), ())), preferred_element_type=jnp.float32)


def _tn(a, b):
    return lax.dot_general(a, b, (((0,), (0,)), ((), ())), preferred_element_type=jnp.float32)


def make_kernel(t_begin, blocks):
    first = t_begin == 0

    def attend_kernel(*refs):
        (q_ref, k_ref, v_ref, pk_ref, kh_ref, vh_ref, pkh_ref, fq_ref, st_ref, z_ref, g_ref, b_ref) = refs[:12]
        if first:
            o_ref, st_out, z_out = refs[12:]
        else:
            o_ref = refs[13]
        heads = q_ref.shape[0]
        head_dim = q_ref.shape[1]
        feats = fq_ref.shape[1]
        half = feats // 2
        inv_scale = 1.0 / jnp.sqrt(jnp.float32(head_dim))
        row = lax.broadcasted_iota(jnp.int32, (feats, QB), 0)
        lo = row < half
        wk = lax.broadcasted_iota(jnp.int32, (2 * QB, QB), 0)
        tq = lax.broadcasted_iota(jnp.int32, (2 * QB, QB), 1)
        win_keep = (wk > tq + WIN) & (wk <= tq + QB)
        lin_keep = wk <= tq + WIN
        zrow = lax.broadcasted_iota(jnp.int32, (8, feats), 0)
        neg = jnp.float32(-1e30)

        def step(hh, t0, st, z, kw, vw, pkw, bias):
            q = q_ref[hh, :, pl.ds(t0 - t_begin, QB)]
            g = g_ref[hh]
            s = jnp.dot(kw, q, preferred_element_type=jnp.float32) * inv_scale
            if bias is not None:
                s = s + bias
            s = jnp.where(win_keep, s, neg)
            top = jnp.max(s, axis=0, keepdims=True)
            p = jnp.exp(s - top)
            total = jnp.sum(p, axis=0, keepdims=True)
            window = jnp.dot(vw, p.astype(jnp.bfloat16), preferred_element_type=jnp.float32)
            window = window * (1.0 / total)

            logits = jnp.dot(fq_ref[hh], q, preferred_element_type=jnp.float32)
            m_lo = jnp.max(logits[:half], axis=0, keepdims=True)
            m_hi = jnp.max(logits[half:], axis=0, keepdims=True)
            e = jnp.exp(logits - jnp.where(lo, m_lo, m_hi))
            s_lo = jnp.sum(e[:half], axis=0, keepdims=True)
            s_hi = jnp.sum(e[half:], axis=0, keepdims=True)
            phi = (e * jnp.where(lo, 1.0 / s_lo, 1.0 / s_hi)).astype(jnp.bfloat16)

            aff = jnp.dot(pkw, phi, preferred_element_type=jnp.float32)
            aff = jnp.where(lin_keep, aff, jnp.float32(0.0)).astype(jnp.bfloat16)
            num = jnp.dot(vw, aff, preferred_element_type=jnp.float32)
            den = jnp.sum(aff.astype(jnp.float32), axis=0, keepdims=True)
            st_hi = st.astype(jnp.bfloat16)
            st_lo = (st - st_hi.astype(jnp.float32)).astype(jnp.bfloat16)
            num = num + jnp.dot(st_hi, phi, preferred_element_type=jnp.float32)
            num = num + jnp.dot(st_lo, phi, preferred_element_type=jnp.float32)
            z_hi = z.astype(jnp.bfloat16)
            z_lo = (z - z_hi.astype(jnp.float32)).astype(jnp.bfloat16)
            zz = jnp.where(zrow == 0, z_hi, jnp.where(zrow == 1, z_lo, jnp.zeros_like(z_lo)))
            cross = jnp.dot(zz, phi, preferred_element_type=jnp.float32)
            den = den + (cross[0:1] + cross[1:2])
            linear = num * (1.0 / (den + 1.0))
            out = g * window + (1.0 - g) * linear
            rows = pl.ds(t0 - t_begin, QB)
            o_ref[rows, pl.ds(hh * head_dim, head_dim)] = out.T.astype(o_ref.dtype)

            vb = vw[:, :QB]
            pkb = pkw[:QB]
            st = st + jnp.dot(vb, pkb, preferred_element_type=jnp.float32)
            z = z + jnp.sum(pkb.astype(jnp.float32), axis=0, keepdims=True)
            return st, z

        carry = []
        for hh in range(heads):
            if first:
                kw0 = jnp.concatenate([kh_ref[hh], k_ref[hh, pl.ds(0, QB), :]], axis=0)
                vw0 = jnp.concatenate([vh_ref[hh], v_ref[hh, :, pl.ds(0, QB)]], axis=1)
                pkw0 = jnp.concatenate([pkh_ref[hh], pk_ref[hh, pl.ds(0, QB), :]], axis=0)
                carry.append(step(hh, 0, st_ref[hh], z_ref[hh][0:1], kw0, vw0, pkw0, b_ref[...]))
            else:
                carry.append((st_ref[hh], z_ref[hh][0:1]))

        def loop(i, carry):
            t0 = pl.multiple_of(i * QB, QB)
            base = pl.multiple_of(t0 - QB, QB)
            out = []
            for hh in range(heads):
                kw = k_ref[hh, pl.ds(base, 2 * QB), :]
                vw = v_ref[hh, :, pl.ds(base, 2 * QB)]
                pkw = pk_ref[hh, pl.ds(base, 2 * QB), :]
                out.append(step(hh, t0, carry[hh][0], carry[hh][1], kw, vw, pkw, None))
            return tuple(out)

        lo_blk = t_begin // QB + (1 if first else 0)
        final = lax.fori_loop(lo_blk, t_begin // QB + blocks, loop, tuple(carry))
        if first:
            for hh in range(heads):
                st_out[hh] = final[hh][0]
                z_out[hh] = jnp.broadcast_to(final[hh][1], (8, feats))

    return attend_kernel


def attend(q, t_begin, k_tm, v, pk, kh, vh, pkh, fq_t, st0, z0, gate_rows, bias0, prev):
    group, head_dim, span = q.shape
    length = v.shape[2]
    feats = fq_t.shape[1]
    hb = HEADS_PER_STEP
    first = prev is None
    in_specs = [
        pl.BlockSpec((hb, head_dim, span), lambda h: (h, 0, 0)),
        pl.BlockSpec((hb, length, head_dim), lambda h: (h, 0, 0)),
        pl.BlockSpec((hb, head_dim, length), lambda h: (h, 0, 0)),
        pl.BlockSpec((hb, length, feats), lambda h: (h, 0, 0)),
        pl.BlockSpec((hb, QB, head_dim), lambda h: (h, 0, 0)),
        pl.BlockSpec((hb, head_dim, QB), lambda h: (h, 0, 0)),
        pl.BlockSpec((hb, QB, feats), lambda h: (h, 0, 0)),
        pl.BlockSpec((hb, feats, head_dim), lambda h: (h, 0, 0)),
        pl.BlockSpec((hb, head_dim, feats), lambda h: (h, 0, 0)),
        pl.BlockSpec((hb, 8, feats), lambda h: (h, 0, 0)),
        pl.BlockSpec((hb, 1, QB), lambda h: (h, 0, 0)),
        pl.BlockSpec((2 * QB, QB), lambda h: (0, 0)),
    ]
    args = [q, k_tm, v, pk, kh, vh, pkh, fq_t, st0, z0, gate_rows, bias0]
    piece = t_begin // span
    out_spec = pl.BlockSpec((span, hb * head_dim), lambda h: (piece, h))
    out_shape = jax.ShapeDtypeStruct((length, group * head_dim), jnp.bfloat16)
    if first:
        out_specs = [
            out_spec,
            pl.BlockSpec((hb, head_dim, feats), lambda h: (h, 0, 0)),
            pl.BlockSpec((hb, 8, feats), lambda h: (h, 0, 0)),
        ]
        out_shapes = [
            out_shape,
            jax.ShapeDtypeStruct(st0.shape, jnp.float32),
            jax.ShapeDtypeStruct(z0.shape, jnp.float32),
        ]
        aliases = {}
    else:
        in_specs.append(pl.BlockSpec(memory_space=pl.ANY))
        args.append(prev)
        out_specs = out_spec
        out_shapes = out_shape
        aliases = {12: 0}
    return pl.pallas_call(
        make_kernel(t_begin, span // QB),
        grid=(group // hb,),
        in_specs=in_specs,
        out_specs=out_specs,
        out_shape=out_shapes,
        input_output_aliases=aliases,
        interpret=INTERPRET,
    )(*args)


def local_part(q_parts, k, v, before, earlier, feat_q, feat_k, prior_state, prior_norm, gate):
    group, head_dim, length = k.shape
    keep = earlier.astype(jnp.bfloat16)
    phi_k = feature_map(k, feat_k)
    phi_halo = feature_map(before[0], feat_k) * keep
    halo_state = jnp.einsum(
        "htf,hdt->hdf", phi_halo, before[1], preferred_element_type=jnp.float32
    )
    halo_norm = jnp.sum(phi_halo, axis=1, dtype=jnp.float32)
    feats = phi_k.shape[2]
    pad_k = jnp.zeros((group, head_dim, QB - WIN), k.dtype)
    kh = jnp.concatenate([pad_k, before[0]], axis=2).transpose(0, 2, 1)
    vh = jnp.concatenate([pad_k, before[1]], axis=2)
    pkh = jnp.concatenate([jnp.zeros((group, QB - WIN, feats), phi_k.dtype), phi_halo], axis=1)
    fq_t = jnp.concatenate([feat_q, -feat_q], axis=2).transpose(0, 2, 1)
    st = prior_state - halo_state
    z = jnp.pad((prior_norm - halo_norm)[:, None, :], ((0, 0), (0, 7), (0, 0)))
    gate_rows = jnp.broadcast_to(gate[:, None, None], (group, 1, QB)).astype(jnp.float32)
    halo_rows = (jnp.arange(2 * QB) >= QB - WIN) & (jnp.arange(2 * QB) < QB)
    bias0 = jnp.where(halo_rows & jnp.logical_not(earlier), jnp.float32(-1e30), jnp.float32(0.0))
    bias0 = jnp.broadcast_to(bias0[:, None], (2 * QB, QB))
    k_tm = k.transpose(0, 2, 1)
    span = q_parts[0].shape[2]
    out, st, z = attend(q_parts[0], 0, k_tm, v, phi_k, kh, vh, pkh, fq_t, st, z, gate_rows, bias0, None)
    for c in range(1, len(q_parts)):
        out = attend(q_parts[c], c * span, k_tm, v, phi_k, kh, vh, pkh, fq_t, st, z, gate_rows, bias0, out)
    return out


def body(queries, keys, values, feat_q, feat_k, mix):
    shards = lax.axis_size("seq")
    place = lax.axis_index("seq")
    feature_rows = queries.shape[0]
    length = queries.shape[1] // shards
    group = feat_q.shape[0]
    head_dim = feat_q.shape[1]

    halves = queries.reshape(feature_rows, shards, Q_PIECES, length // Q_PIECES).transpose(2, 1, 0, 3)
    halves, values = lax.optimization_barrier((halves, values))
    k = exchange(keys.reshape(feature_rows, shards, length), group, head_dim)
    v = exchange(values.reshape(feature_rows, shards, length), group, head_dim)
    q_parts = [
        lax.all_to_all(halves[c], "seq", split_axis=0, concat_axis=0, tiled=True).reshape(
            group, head_dim, -1
        )
        for c in range(Q_PIECES)
    ]

    earlier = place > 0
    tails = jnp.stack([k[:, :, length - WIN :], v[:, :, length - WIN :]])
    before = passed_along(tails, "seq", 1)

    phi_own = feature_map(k, feat_k)
    own_state = jnp.einsum("htf,hdt->hdf", phi_own, v, preferred_element_type=jnp.float32)
    own_norm = jnp.sum(phi_own, axis=1, dtype=jnp.float32)
    own = jnp.concatenate([own_state.reshape(group * head_dim, -1), own_norm], axis=0)
    prior = own
    distance = 1
    while distance < shards:
        prior = prior + passed_along(prior, "seq", distance)
        distance *= 2
    prior = prior - own
    prior_state = prior[: group * head_dim].reshape(own_state.shape)
    prior_norm = prior[group * head_dim :]
    gate = jax.nn.sigmoid(mix)
    return local_part(q_parts, k, v, before, earlier, feat_q, feat_k, prior_state, prior_norm, gate)


def solution(mesh):
    return jax.shard_map(
        body,
        mesh=mesh,
        in_specs=(
            P(("heads", "seq"), None),
            P(("heads", "seq"), None),
            P(("heads", "seq"), None),
            P("heads", None, None),
            P("heads", None, None),
            P("heads"),
        ),
        out_specs=P("seq", "heads"),
        check_vma=False,
    )
```

```python
import functools

import jax
import jax.numpy as jnp
from jax import lax
from jax.experimental import pallas as pl
from jax.experimental.pallas import tpu as pltpu
from jax.sharding import PartitionSpec as P

WIN = 64
QB = 128
HEADS_PER_STEP = 2
Q_PIECES = 2
INTERPRET = False


def passed_along(block, axis, distance):
    devices = range(lax.axis_size(axis))
    route = [(i - distance, i) for i in devices if i - distance in devices]
    return lax.ppermute(block, axis, route)


def exchange(rows, group, head_dim):
    moved = lax.all_to_all(rows, "seq", split_axis=1, concat_axis=0, tiled=True)
    return moved.reshape(group, head_dim, -1)


def feature_map(rows, weight):
    logits = jnp.einsum("hdt,hdf->htf", rows, weight, preferred_element_type=jnp.float32)
    halves = [jax.nn.softmax(logits, axis=-1), jax.nn.softmax(-logits, axis=-1)]
    return jnp.concatenate(halves, axis=-1).astype(jnp.bfloat16)


def _nt(a, b):
    return lax.dot_general(a, b, (((1,), (1,)), ((), ())), preferred_element_type=jnp.float32)


def _tn(a, b):
    return lax.dot_general(a, b, (((0,), (0,)), ((), ())), preferred_element_type=jnp.float32)


def make_kernel(t_begin, blocks):
    first = t_begin == 0

    def attend_kernel(*refs):
        (q_ref, k_ref, v_ref, pk_ref, kh_ref, vh_ref, pkh_ref, fq_ref, st_ref, z_ref, g_ref, b_ref) = refs[:12]
        if first:
            o_ref, st_out, z_out = refs[12:]
        else:
            o_ref = refs[13]
        heads = q_ref.shape[0]
        head_dim = q_ref.shape[1]
        feats = fq_ref.shape[1]
        half = feats // 2
        inv_scale = 1.0 / jnp.sqrt(jnp.float32(head_dim))
        row = lax.broadcasted_iota(jnp.int32, (feats, QB), 0)
        lo = row < half
        wk = lax.broadcasted_iota(jnp.int32, (2 * QB, QB), 0)
        tq = lax.broadcasted_iota(jnp.int32, (2 * QB, QB), 1)
        win_keep = (wk > tq + WIN) & (wk <= tq + QB)
        lin_keep = wk <= tq + WIN
        zrow = lax.broadcasted_iota(jnp.int32, (8, feats), 0)
        neg = jnp.float32(-1e30)

        def step(hh, t0, st, z, kw, vw, pkw, bias):
            q = q_ref[hh, :, pl.ds(t0 - t_begin, QB)]
            g = g_ref[hh]
            s = jnp.dot(kw, q, preferred_element_type=jnp.float32) * inv_scale
            if bias is not None:
                s = s + bias
            s = jnp.where(win_keep, s, neg)
            top = jnp.max(s, axis=0, keepdims=True)
            p = jnp.exp(s - top)
            total = jnp.sum(p, axis=0, keepdims=True)
            window = jnp.dot(vw, p.astype(jnp.bfloat16), preferred_element_type=jnp.float32)
            window = window * (1.0 / total)

            logits = jnp.dot(fq_ref[hh], q, preferred_element_type=jnp.float32)
            m_lo = jnp.max(logits[:half], axis=0, keepdims=True)
            m_hi = jnp.max(logits[half:], axis=0, keepdims=True)
            e = jnp.exp(logits - jnp.where(lo, m_lo, m_hi))
            s_lo = jnp.sum(e[:half], axis=0, keepdims=True)
            s_hi = jnp.sum(e[half:], axis=0, keepdims=True)
            phi = (e * jnp.where(lo, 1.0 / s_lo, 1.0 / s_hi)).astype(jnp.bfloat16)

            aff = jnp.dot(pkw, phi, preferred_element_type=jnp.float32)
            aff = jnp.where(lin_keep, aff, jnp.float32(0.0)).astype(jnp.bfloat16)
            num = jnp.dot(vw, aff, preferred_element_type=jnp.float32)
            den = jnp.sum(aff.astype(jnp.float32), axis=0, keepdims=True)
            st_hi = st.astype(jnp.bfloat16)
            st_lo = (st - st_hi.astype(jnp.float32)).astype(jnp.bfloat16)
            num = num + jnp.dot(st_hi, phi, preferred_element_type=jnp.float32)
            num = num + jnp.dot(st_lo, phi, preferred_element_type=jnp.float32)
            z_hi = z.astype(jnp.bfloat16)
            z_lo = (z - z_hi.astype(jnp.float32)).astype(jnp.bfloat16)
            zz = jnp.where(zrow == 0, z_hi, jnp.where(zrow == 1, z_lo, jnp.zeros_like(z_lo)))
            cross = jnp.dot(zz, phi, preferred_element_type=jnp.float32)
            den = den + (cross[0:1] + cross[1:2])
            linear = num * (1.0 / (den + 1.0))
            out = g * window + (1.0 - g) * linear
            rows = pl.ds(t0 - t_begin, QB)
            o_ref[rows, pl.ds(hh * head_dim, head_dim)] = out.T.astype(o_ref.dtype)

            vb = vw[:, :QB]
            pkb = pkw[:QB]
            st = st + jnp.dot(vb, pkb, preferred_element_type=jnp.float32)
            z = z + jnp.sum(pkb.astype(jnp.float32), axis=0, keepdims=True)
            return st, z

        carry = []
        for hh in range(heads):
            if first:
                kw0 = jnp.concatenate([kh_ref[hh], k_ref[hh, pl.ds(0, QB), :]], axis=0)
                vw0 = jnp.concatenate([vh_ref[hh], v_ref[hh, :, pl.ds(0, QB)]], axis=1)
                pkw0 = jnp.concatenate([pkh_ref[hh], pk_ref[hh, pl.ds(0, QB), :]], axis=0)
                carry.append(step(hh, 0, st_ref[hh], z_ref[hh][0:1], kw0, vw0, pkw0, b_ref[...]))
            else:
                carry.append((st_ref[hh], z_ref[hh][0:1]))

        def loop(i, carry):
            t0 = pl.multiple_of(i * QB, QB)
            base = pl.multiple_of(t0 - QB, QB)
            out = []
            for hh in range(heads):
                kw = k_ref[hh, pl.ds(base, 2 * QB), :]
                vw = v_ref[hh, :, pl.ds(base, 2 * QB)]
                pkw = pk_ref[hh, pl.ds(base, 2 * QB), :]
                out.append(step(hh, t0, carry[hh][0], carry[hh][1], kw, vw, pkw, None))
            return tuple(out)

        lo_blk = t_begin // QB + (1 if first else 0)
        final = lax.fori_loop(lo_blk, t_begin // QB + blocks, loop, tuple(carry))
        if first:
            for hh in range(heads):
                st_out[hh] = final[hh][0]
                z_out[hh] = jnp.broadcast_to(final[hh][1], (8, feats))

    return attend_kernel


def attend(q, t_begin, k_tm, v, pk, kh, vh, pkh, fq_t, st0, z0, gate_rows, bias0, prev):
    group, head_dim, span = q.shape
    length = v.shape[2]
    feats = fq_t.shape[1]
    hb = HEADS_PER_STEP
    first = prev is None
    in_specs = [
        pl.BlockSpec((hb, head_dim, span), lambda h: (h, 0, 0)),
        pl.BlockSpec((hb, length, head_dim), lambda h: (h, 0, 0)),
        pl.BlockSpec((hb, head_dim, length), lambda h: (h, 0, 0)),
        pl.BlockSpec((hb, length, feats), lambda h: (h, 0, 0)),
        pl.BlockSpec((hb, QB, head_dim), lambda h: (h, 0, 0)),
        pl.BlockSpec((hb, head_dim, QB), lambda h: (h, 0, 0)),
        pl.BlockSpec((hb, QB, feats), lambda h: (h, 0, 0)),
        pl.BlockSpec((hb, feats, head_dim), lambda h: (h, 0, 0)),
        pl.BlockSpec((hb, head_dim, feats), lambda h: (h, 0, 0)),
        pl.BlockSpec((hb, 8, feats), lambda h: (h, 0, 0)),
        pl.BlockSpec((hb, 1, QB), lambda h: (h, 0, 0)),
        pl.BlockSpec((2 * QB, QB), lambda h: (0, 0)),
    ]
    args = [q, k_tm, v, pk, kh, vh, pkh, fq_t, st0, z0, gate_rows, bias0]
    piece = t_begin // span
    out_spec = pl.BlockSpec((span, hb * head_dim), lambda h: (piece, h))
    out_shape = jax.ShapeDtypeStruct((length, group * head_dim), jnp.bfloat16)
    if first:
        out_specs = [
            out_spec,
            pl.BlockSpec((hb, head_dim, feats), lambda h: (h, 0, 0)),
            pl.BlockSpec((hb, 8, feats), lambda h: (h, 0, 0)),
        ]
        out_shapes = [
            out_shape,
            jax.ShapeDtypeStruct(st0.shape, jnp.float32),
            jax.ShapeDtypeStruct(z0.shape, jnp.float32),
        ]
        aliases = {}
    else:
        in_specs.append(pl.BlockSpec(memory_space=pl.ANY))
        args.append(prev)
        out_specs = out_spec
        out_shapes = out_shape
        aliases = {12: 0}
    return pl.pallas_call(
        make_kernel(t_begin, span // QB),
        grid=(group // hb,),
        in_specs=in_specs,
        out_specs=out_specs,
        out_shape=out_shapes,
        input_output_aliases=aliases,
        interpret=INTERPRET,
    )(*args)


def local_part(q_parts, k, v, before, earlier, feat_q, feat_k, prior_state, prior_norm, gate):
    group, head_dim, length = k.shape
    keep = earlier.astype(jnp.bfloat16)
    phi_k = feature_map(k, feat_k)
    phi_halo = feature_map(before[0], feat_k) * keep
    halo_state = jnp.einsum(
        "htf,hdt->hdf", phi_halo, before[1], preferred_element_type=jnp.float32
    )
    halo_norm = jnp.sum(phi_halo, axis=1, dtype=jnp.float32)
    feats = phi_k.shape[2]
    pad_k = jnp.zeros((group, head_dim, QB - WIN), k.dtype)
    kh = jnp.concatenate([pad_k, before[0]], axis=2).transpose(0, 2, 1)
    vh = jnp.concatenate([pad_k, before[1]], axis=2)
    pkh = jnp.concatenate([jnp.zeros((group, QB - WIN, feats), phi_k.dtype), phi_halo], axis=1)
    fq_t = jnp.concatenate([feat_q, -feat_q], axis=2).transpose(0, 2, 1)
    st = prior_state - halo_state
    z = jnp.pad((prior_norm - halo_norm)[:, None, :], ((0, 0), (0, 7), (0, 0)))
    gate_rows = jnp.broadcast_to(gate[:, None, None], (group, 1, QB)).astype(jnp.float32)
    halo_rows = (jnp.arange(2 * QB) >= QB - WIN) & (jnp.arange(2 * QB) < QB)
    bias0 = jnp.where(halo_rows & jnp.logical_not(earlier), jnp.float32(-1e30), jnp.float32(0.0))
    bias0 = jnp.broadcast_to(bias0[:, None], (2 * QB, QB))
    k_tm = k.transpose(0, 2, 1)
    span = q_parts[0].shape[2]
    out, st, z = attend(q_parts[0], 0, k_tm, v, phi_k, kh, vh, pkh, fq_t, st, z, gate_rows, bias0, None)
    for c in range(1, len(q_parts)):
        out = attend(q_parts[c], c * span, k_tm, v, phi_k, kh, vh, pkh, fq_t, st, z, gate_rows, bias0, out)
    return out


def body(queries, keys, values, feat_q, feat_k, mix):
    shards = lax.axis_size("seq")
    place = lax.axis_index("seq")
    feature_rows = queries.shape[0]
    length = queries.shape[1] // shards
    group = feat_q.shape[0]
    head_dim = feat_q.shape[1]

    halves = queries.reshape(feature_rows, shards, Q_PIECES, length // Q_PIECES).transpose(2, 1, 0, 3)
    halves, values = lax.optimization_barrier((halves, values))
    k = exchange(keys.reshape(feature_rows, shards, length), group, head_dim)
    v = exchange(values.reshape(feature_rows, shards, length), group, head_dim)
    q_parts = [
        lax.all_to_all(halves[c], "seq", split_axis=0, concat_axis=0, tiled=True).reshape(
            group, head_dim, -1
        )
        for c in range(Q_PIECES)
    ]

    earlier = place > 0
    tails = jnp.stack([k[:, :, length - WIN :], v[:, :, length - WIN :]])
    before = passed_along(tails, "seq", 1)

    phi_own = feature_map(k, feat_k)
    own_state = jnp.einsum("htf,hdt->hdf", phi_own, v, preferred_element_type=jnp.float32)
    own_norm = jnp.sum(phi_own, axis=1, dtype=jnp.float32)
    own = jnp.concatenate([own_state.reshape(group * head_dim, -1), own_norm], axis=0)
    prior = own
    distance = 1
    while distance < shards:
        prior = prior + passed_along(prior.astype(jnp.bfloat16), "seq", distance).astype(jnp.float32)
        distance *= 2
    prior = prior - own
    prior_state = prior[: group * head_dim].reshape(own_state.shape)
    prior_norm = prior[group * head_dim :]
    gate = jax.nn.sigmoid(mix)
    return local_part(q_parts, k, v, before, earlier, feat_q, feat_k, prior_state, prior_norm, gate)


def solution(mesh):
    return jax.shard_map(
        body,
        mesh=mesh,
        in_specs=(
            P(("heads", "seq"), None),
            P(("heads", "seq"), None),
            P(("heads", "seq"), None),
            P("heads", None, None),
            P("heads", None, None),
            P("heads"),
        ),
        out_specs=P("seq", "heads"),
        check_vma=False,
    )
```

```python
import functools

import jax
import jax.numpy as jnp
from jax import lax
from jax.experimental import pallas as pl
from jax.experimental.pallas import tpu as pltpu
from jax.sharding import PartitionSpec as P

WIN = 64
QB = 128
HEADS_PER_STEP = 2
Q_PIECES = 2
UNROLL = 2
INTERPRET = False


def passed_along(block, axis, distance):
    devices = range(lax.axis_size(axis))
    route = [(i - distance, i) for i in devices if i - distance in devices]
    return lax.ppermute(block, axis, route)


def exchange(rows, group, head_dim):
    moved = lax.all_to_all(rows, "seq", split_axis=1, concat_axis=0, tiled=True)
    return moved.reshape(group, head_dim, -1)


def feature_map(rows, weight):
    logits = jnp.einsum("hdt,hdf->htf", rows, weight, preferred_element_type=jnp.float32)
    halves = [jax.nn.softmax(logits, axis=-1), jax.nn.softmax(-logits, axis=-1)]
    return jnp.concatenate(halves, axis=-1).astype(jnp.bfloat16)


def _nt(a, b):
    return lax.dot_general(a, b, (((1,), (1,)), ((), ())), preferred_element_type=jnp.float32)


def _tn(a, b):
    return lax.dot_general(a, b, (((0,), (0,)), ((), ())), preferred_element_type=jnp.float32)


def make_kernel(t_begin, blocks):
    first = t_begin == 0

    def attend_kernel(*refs):
        (q_ref, k_ref, v_ref, pk_ref, kh_ref, vh_ref, pkh_ref, fq_ref, st_ref, z_ref, g_ref, b_ref) = refs[:12]
        if first:
            o_ref, st_out, z_out = refs[12:]
        else:
            o_ref = refs[13]
        heads = q_ref.shape[0]
        head_dim = q_ref.shape[1]
        feats = fq_ref.shape[1]
        half = feats // 2
        inv_scale = 1.0 / jnp.sqrt(jnp.float32(head_dim))
        row = lax.broadcasted_iota(jnp.int32, (feats, QB), 0)
        lo = row < half
        wk = lax.broadcasted_iota(jnp.int32, (2 * QB, QB), 0)
        tq = lax.broadcasted_iota(jnp.int32, (2 * QB, QB), 1)
        win_keep = (wk > tq + WIN) & (wk <= tq + QB)
        lin_keep = wk <= tq + WIN
        zrow = lax.broadcasted_iota(jnp.int32, (8, feats), 0)
        neg = jnp.float32(-1e30)

        def step(hh, t0, st, z, kw, vw, pkw, bias):
            q = q_ref[hh, :, pl.ds(t0 - t_begin, QB)]
            g = g_ref[hh]
            s = jnp.dot(kw, q, preferred_element_type=jnp.float32) * inv_scale
            if bias is not None:
                s = s + bias
            s = jnp.where(win_keep, s, neg)
            top = jnp.max(s, axis=0, keepdims=True)
            p = jnp.exp(s - top)
            total = jnp.sum(p, axis=0, keepdims=True)
            window = jnp.dot(vw, p.astype(jnp.bfloat16), preferred_element_type=jnp.float32)
            window = window * (1.0 / total)

            logits = jnp.dot(fq_ref[hh], q, preferred_element_type=jnp.float32)
            m_lo = jnp.max(logits[:half], axis=0, keepdims=True)
            m_hi = jnp.max(logits[half:], axis=0, keepdims=True)
            e = jnp.exp(logits - jnp.where(lo, m_lo, m_hi))
            s_lo = jnp.sum(e[:half], axis=0, keepdims=True)
            s_hi = jnp.sum(e[half:], axis=0, keepdims=True)
            phi = (e * jnp.where(lo, 1.0 / s_lo, 1.0 / s_hi)).astype(jnp.bfloat16)

            aff = jnp.dot(pkw, phi, preferred_element_type=jnp.float32)
            aff = jnp.where(lin_keep, aff, jnp.float32(0.0)).astype(jnp.bfloat16)
            num = jnp.dot(vw, aff, preferred_element_type=jnp.float32)
            den = jnp.sum(aff.astype(jnp.float32), axis=0, keepdims=True)
            st_hi = st.astype(jnp.bfloat16)
            st_lo = (st - st_hi.astype(jnp.float32)).astype(jnp.bfloat16)
            num = num + jnp.dot(st_hi, phi, preferred_element_type=jnp.float32)
            num = num + jnp.dot(st_lo, phi, preferred_element_type=jnp.float32)
            z_hi = z.astype(jnp.bfloat16)
            z_lo = (z - z_hi.astype(jnp.float32)).astype(jnp.bfloat16)
            zz = jnp.where(zrow == 0, z_hi, jnp.where(zrow == 1, z_lo, jnp.zeros_like(z_lo)))
            cross = jnp.dot(zz, phi, preferred_element_type=jnp.float32)
            den = den + (cross[0:1] + cross[1:2])
            linear = num * (1.0 / (den + 1.0))
            out = g * window + (1.0 - g) * linear
            rows = pl.ds(t0 - t_begin, QB)
            o_ref[rows, pl.ds(hh * head_dim, head_dim)] = out.T.astype(o_ref.dtype)

            vb = vw[:, :QB]
            pkb = pkw[:QB]
            st = st + jnp.dot(vb, pkb, preferred_element_type=jnp.float32)
            z = z + jnp.sum(pkb.astype(jnp.float32), axis=0, keepdims=True)
            return st, z

        carry = []
        for hh in range(heads):
            if first:
                kw0 = jnp.concatenate([kh_ref[hh], k_ref[hh, pl.ds(0, QB), :]], axis=0)
                vw0 = jnp.concatenate([vh_ref[hh], v_ref[hh, :, pl.ds(0, QB)]], axis=1)
                pkw0 = jnp.concatenate([pkh_ref[hh], pk_ref[hh, pl.ds(0, QB), :]], axis=0)
                carry.append(step(hh, 0, st_ref[hh], z_ref[hh][0:1], kw0, vw0, pkw0, b_ref[...]))
            else:
                carry.append((st_ref[hh], z_ref[hh][0:1]))

        def one(t0, carry):
            base = t0 - QB
            out = []
            for hh in range(heads):
                kw = k_ref[hh, pl.ds(base, 2 * QB), :]
                vw = v_ref[hh, :, pl.ds(base, 2 * QB)]
                pkw = pk_ref[hh, pl.ds(base, 2 * QB), :]
                out.append(step(hh, t0, carry[hh][0], carry[hh][1], kw, vw, pkw, None))
            return tuple(out)

        lo_blk = t_begin // QB + (1 if first else 0)
        hi_blk = t_begin // QB + blocks
        pairs = (hi_blk - lo_blk) // UNROLL

        def loop(i, carry):
            for u in range(UNROLL):
                t0 = pl.multiple_of((lo_blk + i * UNROLL + u) * QB, QB)
                carry = one(t0, carry)
            return carry

        final = lax.fori_loop(0, pairs, loop, tuple(carry))
        for blk in range(lo_blk + pairs * UNROLL, hi_blk):
            final = one(blk * QB, final)
        if first:
            for hh in range(heads):
                st_out[hh] = final[hh][0]
                z_out[hh] = jnp.broadcast_to(final[hh][1], (8, feats))

    return attend_kernel


def attend(q, t_begin, k_tm, v, pk, kh, vh, pkh, fq_t, st0, z0, gate_rows, bias0, prev):
    group, head_dim, span = q.shape
    length = v.shape[2]
    feats = fq_t.shape[1]
    hb = HEADS_PER_STEP
    first = prev is None
    in_specs = [
        pl.BlockSpec((hb, head_dim, span), lambda h: (h, 0, 0)),
        pl.BlockSpec((hb, length, head_dim), lambda h: (h, 0, 0)),
        pl.BlockSpec((hb, head_dim, length), lambda h: (h, 0, 0)),
        pl.BlockSpec((hb, length, feats), lambda h: (h, 0, 0)),
        pl.BlockSpec((hb, QB, head_dim), lambda h: (h, 0, 0)),
        pl.BlockSpec((hb, head_dim, QB), lambda h: (h, 0, 0)),
        pl.BlockSpec((hb, QB, feats), lambda h: (h, 0, 0)),
        pl.BlockSpec((hb, feats, head_dim), lambda h: (h, 0, 0)),
        pl.BlockSpec((hb, head_dim, feats), lambda h: (h, 0, 0)),
        pl.BlockSpec((hb, 8, feats), lambda h: (h, 0, 0)),
        pl.BlockSpec((hb, 1, QB), lambda h: (h, 0, 0)),
        pl.BlockSpec((2 * QB, QB), lambda h: (0, 0)),
    ]
    args = [q, k_tm, v, pk, kh, vh, pkh, fq_t, st0, z0, gate_rows, bias0]
    piece = t_begin // span
    out_spec = pl.BlockSpec((span, hb * head_dim), lambda h: (piece, h))
    out_shape = jax.ShapeDtypeStruct((length, group * head_dim), jnp.bfloat16)
    if first:
        out_specs = [
            out_spec,
            pl.BlockSpec((hb, head_dim, feats), lambda h: (h, 0, 0)),
            pl.BlockSpec((hb, 8, feats), lambda h: (h, 0, 0)),
        ]
        out_shapes = [
            out_shape,
            jax.ShapeDtypeStruct(st0.shape, jnp.float32),
            jax.ShapeDtypeStruct(z0.shape, jnp.float32),
        ]
        aliases = {}
    else:
        in_specs.append(pl.BlockSpec(memory_space=pl.ANY))
        args.append(prev)
        out_specs = out_spec
        out_shapes = out_shape
        aliases = {12: 0}
    return pl.pallas_call(
        make_kernel(t_begin, span // QB),
        grid=(group // hb,),
        in_specs=in_specs,
        out_specs=out_specs,
        out_shape=out_shapes,
        input_output_aliases=aliases,
        interpret=INTERPRET,
    )(*args)


def local_part(q_parts, k, v, before, earlier, feat_q, feat_k, prior_state, prior_norm, gate):
    group, head_dim, length = k.shape
    keep = earlier.astype(jnp.bfloat16)
    phi_k = feature_map(k, feat_k)
    phi_halo = feature_map(before[0], feat_k) * keep
    halo_state = jnp.einsum(
        "htf,hdt->hdf", phi_halo, before[1], preferred_element_type=jnp.float32
    )
    halo_norm = jnp.sum(phi_halo, axis=1, dtype=jnp.float32)
    feats = phi_k.shape[2]
    pad_k = jnp.zeros((group, head_dim, QB - WIN), k.dtype)
    kh = jnp.concatenate([pad_k, before[0]], axis=2).transpose(0, 2, 1)
    vh = jnp.concatenate([pad_k, before[1]], axis=2)
    pkh = jnp.concatenate([jnp.zeros((group, QB - WIN, feats), phi_k.dtype), phi_halo], axis=1)
    fq_t = jnp.concatenate([feat_q, -feat_q], axis=2).transpose(0, 2, 1)
    st = prior_state - halo_state
    z = jnp.pad((prior_norm - halo_norm)[:, None, :], ((0, 0), (0, 7), (0, 0)))
    gate_rows = jnp.broadcast_to(gate[:, None, None], (group, 1, QB)).astype(jnp.float32)
    halo_rows = (jnp.arange(2 * QB) >= QB - WIN) & (jnp.arange(2 * QB) < QB)
    bias0 = jnp.where(halo_rows & jnp.logical_not(earlier), jnp.float32(-1e30), jnp.float32(0.0))
    bias0 = jnp.broadcast_to(bias0[:, None], (2 * QB, QB))
    k_tm = k.transpose(0, 2, 1)
    span = q_parts[0].shape[2]
    out, st, z = attend(q_parts[0], 0, k_tm, v, phi_k, kh, vh, pkh, fq_t, st, z, gate_rows, bias0, None)
    for c in range(1, len(q_parts)):
        out = attend(q_parts[c], c * span, k_tm, v, phi_k, kh, vh, pkh, fq_t, st, z, gate_rows, bias0, out)
    return out


def body(queries, keys, values, feat_q, feat_k, mix):
    shards = lax.axis_size("seq")
    place = lax.axis_index("seq")
    feature_rows = queries.shape[0]
    length = queries.shape[1] // shards
    group = feat_q.shape[0]
    head_dim = feat_q.shape[1]

    halves = queries.reshape(feature_rows, shards, Q_PIECES, length // Q_PIECES).transpose(2, 1, 0, 3)
    halves, values = lax.optimization_barrier((halves, values))
    k = exchange(keys.reshape(feature_rows, shards, length), group, head_dim)
    v = exchange(values.reshape(feature_rows, shards, length), group, head_dim)
    q_parts = [
        lax.all_to_all(halves[c], "seq", split_axis=0, concat_axis=0, tiled=True).reshape(
            group, head_dim, -1
        )
        for c in range(Q_PIECES)
    ]

    earlier = place > 0
    tails = jnp.stack([k[:, :, length - WIN :], v[:, :, length - WIN :]])
    before = passed_along(tails, "seq", 1)

    phi_own = feature_map(k, feat_k)
    own_state = jnp.einsum("htf,hdt->hdf", phi_own, v, preferred_element_type=jnp.float32)
    own_norm = jnp.sum(phi_own, axis=1, dtype=jnp.float32)
    own = jnp.concatenate([own_state.reshape(group * head_dim, -1), own_norm], axis=0)
    prior = own
    distance = 1
    while distance < shards:
        prior = prior + passed_along(prior.astype(jnp.bfloat16), "seq", distance).astype(jnp.float32)
        distance *= 2
    prior = prior - own
    prior_state = prior[: group * head_dim].reshape(own_state.shape)
    prior_norm = prior[group * head_dim :]
    gate = jax.nn.sigmoid(mix)
    return local_part(q_parts, k, v, before, earlier, feat_q, feat_k, prior_state, prior_norm, gate)


def solution(mesh):
    return jax.shard_map(
        body,
        mesh=mesh,
        in_specs=(
            P(("heads", "seq"), None),
            P(("heads", "seq"), None),
            P(("heads", "seq"), None),
            P("heads", None, None),
            P("heads", None, None),
            P("heads"),
        ),
        out_specs=P("seq", "heads"),
        check_vma=False,
    )
```

```python
import functools

import jax
import jax.numpy as jnp
from jax import lax
from jax.experimental import pallas as pl
from jax.experimental.pallas import tpu as pltpu
from jax.sharding import PartitionSpec as P

WIN = 64
QB = 128
HEADS_PER_STEP = 2
Q_PIECES = 2
UNROLL = 4
INTERPRET = False


def passed_along(block, axis, distance):
    devices = range(lax.axis_size(axis))
    route = [(i - distance, i) for i in devices if i - distance in devices]
    return lax.ppermute(block, axis, route)


def exchange(rows, group, head_dim):
    moved = lax.all_to_all(rows, "seq", split_axis=1, concat_axis=0, tiled=True)
    return moved.reshape(group, head_dim, -1)


def feature_map(rows, weight):
    logits = jnp.einsum("hdt,hdf->htf", rows, weight, preferred_element_type=jnp.float32)
    halves = [jax.nn.softmax(logits, axis=-1), jax.nn.softmax(-logits, axis=-1)]
    return jnp.concatenate(halves, axis=-1).astype(jnp.bfloat16)


def _nt(a, b):
    return lax.dot_general(a, b, (((1,), (1,)), ((), ())), preferred_element_type=jnp.float32)


def _tn(a, b):
    return lax.dot_general(a, b, (((0,), (0,)), ((), ())), preferred_element_type=jnp.float32)


def make_kernel(t_begin, blocks):
    first = t_begin == 0

    def attend_kernel(*refs):
        (q_ref, k_ref, v_ref, pk_ref, kh_ref, vh_ref, pkh_ref, fq_ref, st_ref, z_ref, g_ref, b_ref) = refs[:12]
        if first:
            o_ref, st_out, z_out = refs[12:]
        else:
            o_ref = refs[13]
        heads = q_ref.shape[0]
        head_dim = q_ref.shape[1]
        feats = fq_ref.shape[1]
        half = feats // 2
        inv_scale = 1.0 / jnp.sqrt(jnp.float32(head_dim))
        row = lax.broadcasted_iota(jnp.int32, (feats, QB), 0)
        lo = row < half
        wk = lax.broadcasted_iota(jnp.int32, (2 * QB, QB), 0)
        tq = lax.broadcasted_iota(jnp.int32, (2 * QB, QB), 1)
        win_keep = (wk > tq + WIN) & (wk <= tq + QB)
        lin_keep = wk <= tq + WIN
        zrow = lax.broadcasted_iota(jnp.int32, (8, feats), 0)
        neg = jnp.float32(-1e30)

        def step(hh, t0, st, z, kw, vw, pkw, bias):
            q = q_ref[hh, :, pl.ds(t0 - t_begin, QB)]
            g = g_ref[hh]
            s = jnp.dot(kw, q, preferred_element_type=jnp.float32) * inv_scale
            if bias is not None:
                s = s + bias
            s = jnp.where(win_keep, s, neg)
            top = jnp.max(s, axis=0, keepdims=True)
            p = jnp.exp(s - top)
            total = jnp.sum(p, axis=0, keepdims=True)
            window = jnp.dot(vw, p.astype(jnp.bfloat16), preferred_element_type=jnp.float32)
            window = window * (1.0 / total)

            logits = jnp.dot(fq_ref[hh], q, preferred_element_type=jnp.float32)
            m_lo = jnp.max(logits[:half], axis=0, keepdims=True)
            m_hi = jnp.max(logits[half:], axis=0, keepdims=True)
            e = jnp.exp(logits - jnp.where(lo, m_lo, m_hi))
            s_lo = jnp.sum(e[:half], axis=0, keepdims=True)
            s_hi = jnp.sum(e[half:], axis=0, keepdims=True)
            phi = (e * jnp.where(lo, 1.0 / s_lo, 1.0 / s_hi)).astype(jnp.bfloat16)

            aff = jnp.dot(pkw, phi, preferred_element_type=jnp.float32)
            aff = jnp.where(lin_keep, aff, jnp.float32(0.0)).astype(jnp.bfloat16)
            num = jnp.dot(vw, aff, preferred_element_type=jnp.float32)
            den = jnp.sum(aff.astype(jnp.float32), axis=0, keepdims=True)
            st_hi = st.astype(jnp.bfloat16)
            st_lo = (st - st_hi.astype(jnp.float32)).astype(jnp.bfloat16)
            num = num + jnp.dot(st_hi, phi, preferred_element_type=jnp.float32)
            num = num + jnp.dot(st_lo, phi, preferred_element_type=jnp.float32)
            z_hi = z.astype(jnp.bfloat16)
            z_lo = (z - z_hi.astype(jnp.float32)).astype(jnp.bfloat16)
            zz = jnp.where(zrow == 0, z_hi, jnp.where(zrow == 1, z_lo, jnp.zeros_like(z_lo)))
            cross = jnp.dot(zz, phi, preferred_element_type=jnp.float32)
            den = den + (cross[0:1] + cross[1:2])
            linear = num * (1.0 / (den + 1.0))
            out = g * window + (1.0 - g) * linear
            rows = pl.ds(t0 - t_begin, QB)
            o_ref[rows, pl.ds(hh * head_dim, head_dim)] = out.T.astype(o_ref.dtype)

            vb = vw[:, :QB]
            pkb = pkw[:QB]
            st = st + jnp.dot(vb, pkb, preferred_element_type=jnp.float32)
            z = z + jnp.sum(pkb.astype(jnp.float32), axis=0, keepdims=True)
            return st, z

        carry = []
        for hh in range(heads):
            if first:
                kw0 = jnp.concatenate([kh_ref[hh], k_ref[hh, pl.ds(0, QB), :]], axis=0)
                vw0 = jnp.concatenate([vh_ref[hh], v_ref[hh, :, pl.ds(0, QB)]], axis=1)
                pkw0 = jnp.concatenate([pkh_ref[hh], pk_ref[hh, pl.ds(0, QB), :]], axis=0)
                carry.append(step(hh, 0, st_ref[hh], z_ref[hh][0:1], kw0, vw0, pkw0, b_ref[...]))
            else:
                carry.append((st_ref[hh], z_ref[hh][0:1]))

        def one(t0, carry):
            base = t0 - QB
            out = []
            for hh in range(heads):
                kw = k_ref[hh, pl.ds(base, 2 * QB), :]
                vw = v_ref[hh, :, pl.ds(base, 2 * QB)]
                pkw = pk_ref[hh, pl.ds(base, 2 * QB), :]
                out.append(step(hh, t0, carry[hh][0], carry[hh][1], kw, vw, pkw, None))
            return tuple(out)

        lo_blk = t_begin // QB + (1 if first else 0)
        hi_blk = t_begin // QB + blocks
        pairs = (hi_blk - lo_blk) // UNROLL

        def loop(i, carry):
            for u in range(UNROLL):
                t0 = pl.multiple_of((lo_blk + i * UNROLL + u) * QB, QB)
                carry = one(t0, carry)
            return carry

        final = lax.fori_loop(0, pairs, loop, tuple(carry))
        for blk in range(lo_blk + pairs * UNROLL, hi_blk):
            final = one(blk * QB, final)
        if first:
            for hh in range(heads):
                st_out[hh] = final[hh][0]
                z_out[hh] = jnp.broadcast_to(final[hh][1], (8, feats))

    return attend_kernel


def attend(q, t_begin, k_tm, v, pk, kh, vh, pkh, fq_t, st0, z0, gate_rows, bias0, prev):
    group, head_dim, span = q.shape
    length = v.shape[2]
    feats = fq_t.shape[1]
    hb = HEADS_PER_STEP
    first = prev is None
    in_specs = [
        pl.BlockSpec((hb, head_dim, span), lambda h: (h, 0, 0)),
        pl.BlockSpec((hb, length, head_dim), lambda h: (h, 0, 0)),
        pl.BlockSpec((hb, head_dim, length), lambda h: (h, 0, 0)),
        pl.BlockSpec((hb, length, feats), lambda h: (h, 0, 0)),
        pl.BlockSpec((hb, QB, head_dim), lambda h: (h, 0, 0)),
        pl.BlockSpec((hb, head_dim, QB), lambda h: (h, 0, 0)),
        pl.BlockSpec((hb, QB, feats), lambda h: (h, 0, 0)),
        pl.BlockSpec((hb, feats, head_dim), lambda h: (h, 0, 0)),
        pl.BlockSpec((hb, head_dim, feats), lambda h: (h, 0, 0)),
        pl.BlockSpec((hb, 8, feats), lambda h: (h, 0, 0)),
        pl.BlockSpec((hb, 1, QB), lambda h: (h, 0, 0)),
        pl.BlockSpec((2 * QB, QB), lambda h: (0, 0)),
    ]
    args = [q, k_tm, v, pk, kh, vh, pkh, fq_t, st0, z0, gate_rows, bias0]
    piece = t_begin // span
    out_spec = pl.BlockSpec((span, hb * head_dim), lambda h: (piece, h))
    out_shape = jax.ShapeDtypeStruct((length, group * head_dim), jnp.bfloat16)
    if first:
        out_specs = [
            out_spec,
            pl.BlockSpec((hb, head_dim, feats), lambda h: (h, 0, 0)),
            pl.BlockSpec((hb, 8, feats), lambda h: (h, 0, 0)),
        ]
        out_shapes = [
            out_shape,
            jax.ShapeDtypeStruct(st0.shape, jnp.float32),
            jax.ShapeDtypeStruct(z0.shape, jnp.float32),
        ]
        aliases = {}
    else:
        in_specs.append(pl.BlockSpec(memory_space=pl.ANY))
        args.append(prev)
        out_specs = out_spec
        out_shapes = out_shape
        aliases = {12: 0}
    return pl.pallas_call(
        make_kernel(t_begin, span // QB),
        grid=(group // hb,),
        in_specs=in_specs,
        out_specs=out_specs,
        out_shape=out_shapes,
        input_output_aliases=aliases,
        interpret=INTERPRET,
    )(*args)


def local_part(q_parts, k, v, before, earlier, feat_q, feat_k, prior_state, prior_norm, gate):
    group, head_dim, length = k.shape
    keep = earlier.astype(jnp.bfloat16)
    phi_k = feature_map(k, feat_k)
    phi_halo = feature_map(before[0], feat_k) * keep
    halo_state = jnp.einsum(
        "htf,hdt->hdf", phi_halo, before[1], preferred_element_type=jnp.float32
    )
    halo_norm = jnp.sum(phi_halo, axis=1, dtype=jnp.float32)
    feats = phi_k.shape[2]
    pad_k = jnp.zeros((group, head_dim, QB - WIN), k.dtype)
    kh = jnp.concatenate([pad_k, before[0]], axis=2).transpose(0, 2, 1)
    vh = jnp.concatenate([pad_k, before[1]], axis=2)
    pkh = jnp.concatenate([jnp.zeros((group, QB - WIN, feats), phi_k.dtype), phi_halo], axis=1)
    fq_t = jnp.concatenate([feat_q, -feat_q], axis=2).transpose(0, 2, 1)
    st = prior_state - halo_state
    z = jnp.pad((prior_norm - halo_norm)[:, None, :], ((0, 0), (0, 7), (0, 0)))
    gate_rows = jnp.broadcast_to(gate[:, None, None], (group, 1, QB)).astype(jnp.float32)
    halo_rows = (jnp.arange(2 * QB) >= QB - WIN) & (jnp.arange(2 * QB) < QB)
    bias0 = jnp.where(halo_rows & jnp.logical_not(earlier), jnp.float32(-1e30), jnp.float32(0.0))
    bias0 = jnp.broadcast_to(bias0[:, None], (2 * QB, QB))
    k_tm = k.transpose(0, 2, 1)
    span = q_parts[0].shape[2]
    out, st, z = attend(q_parts[0], 0, k_tm, v, phi_k, kh, vh, pkh, fq_t, st, z, gate_rows, bias0, None)
    for c in range(1, len(q_parts)):
        out = attend(q_parts[c], c * span, k_tm, v, phi_k, kh, vh, pkh, fq_t, st, z, gate_rows, bias0, out)
    return out


def body(queries, keys, values, feat_q, feat_k, mix):
    shards = lax.axis_size("seq")
    place = lax.axis_index("seq")
    feature_rows = queries.shape[0]
    length = queries.shape[1] // shards
    group = feat_q.shape[0]
    head_dim = feat_q.shape[1]

    halves = queries.reshape(feature_rows, shards, Q_PIECES, length // Q_PIECES).transpose(2, 1, 0, 3)
    halves, values = lax.optimization_barrier((halves, values))
    k = exchange(keys.reshape(feature_rows, shards, length), group, head_dim)
    v = exchange(values.reshape(feature_rows, shards, length), group, head_dim)
    q_parts = [
        lax.all_to_all(halves[c], "seq", split_axis=0, concat_axis=0, tiled=True).reshape(
            group, head_dim, -1
        )
        for c in range(Q_PIECES)
    ]

    earlier = place > 0
    tails = jnp.stack([k[:, :, length - WIN :], v[:, :, length - WIN :]])
    before = passed_along(tails, "seq", 1)

    phi_own = feature_map(k, feat_k)
    own_state = jnp.einsum("htf,hdt->hdf", phi_own, v, preferred_element_type=jnp.float32)
    own_norm = jnp.sum(phi_own, axis=1, dtype=jnp.float32)
    own = jnp.concatenate([own_state.reshape(group * head_dim, -1), own_norm], axis=0)
    prior = own
    distance = 1
    while distance < shards:
        prior = prior + passed_along(prior.astype(jnp.bfloat16), "seq", distance).astype(jnp.float32)
        distance *= 2
    prior = prior - own
    prior_state = prior[: group * head_dim].reshape(own_state.shape)
    prior_norm = prior[group * head_dim :]
    gate = jax.nn.sigmoid(mix)
    return local_part(q_parts, k, v, before, earlier, feat_q, feat_k, prior_state, prior_norm, gate)


def solution(mesh):
    return jax.shard_map(
        body,
        mesh=mesh,
        in_specs=(
            P(("heads", "seq"), None),
            P(("heads", "seq"), None),
            P(("heads", "seq"), None),
            P("heads", None, None),
            P("heads", None, None),
            P("heads"),
        ),
        out_specs=P("seq", "heads"),
        check_vma=False,
    )
```

```python
import functools

import jax
import jax.numpy as jnp
from jax import lax
from jax.experimental import pallas as pl
from jax.experimental.pallas import tpu as pltpu
from jax.sharding import PartitionSpec as P

WIN = 64
QB = 128
HEADS_PER_STEP = 2
Q_PIECES = 2
UNROLL = 8
INTERPRET = False


def passed_along(block, axis, distance):
    devices = range(lax.axis_size(axis))
    route = [(i - distance, i) for i in devices if i - distance in devices]
    return lax.ppermute(block, axis, route)


def exchange(rows, group, head_dim):
    moved = lax.all_to_all(rows, "seq", split_axis=1, concat_axis=0, tiled=True)
    return moved.reshape(group, head_dim, -1)


def feature_map(rows, weight):
    logits = jnp.einsum("hdt,hdf->htf", rows, weight, preferred_element_type=jnp.float32)
    halves = [jax.nn.softmax(logits, axis=-1), jax.nn.softmax(-logits, axis=-1)]
    return jnp.concatenate(halves, axis=-1).astype(jnp.bfloat16)


def _nt(a, b):
    return lax.dot_general(a, b, (((1,), (1,)), ((), ())), preferred_element_type=jnp.float32)


def _tn(a, b):
    return lax.dot_general(a, b, (((0,), (0,)), ((), ())), preferred_element_type=jnp.float32)


def make_kernel(t_begin, blocks):
    first = t_begin == 0

    def attend_kernel(*refs):
        (q_ref, k_ref, v_ref, pk_ref, kh_ref, vh_ref, pkh_ref, fq_ref, st_ref, z_ref, g_ref, b_ref) = refs[:12]
        if first:
            o_ref, st_out, z_out = refs[12:]
        else:
            o_ref = refs[13]
        heads = q_ref.shape[0]
        head_dim = q_ref.shape[1]
        feats = fq_ref.shape[1]
        half = feats // 2
        inv_scale = 1.0 / jnp.sqrt(jnp.float32(head_dim))
        row = lax.broadcasted_iota(jnp.int32, (feats, QB), 0)
        lo = row < half
        wk = lax.broadcasted_iota(jnp.int32, (2 * QB, QB), 0)
        tq = lax.broadcasted_iota(jnp.int32, (2 * QB, QB), 1)
        win_keep = (wk > tq + WIN) & (wk <= tq + QB)
        lin_keep = wk <= tq + WIN
        zrow = lax.broadcasted_iota(jnp.int32, (8, feats), 0)
        neg = jnp.float32(-1e30)

        def step(hh, t0, st, z, kw, vw, pkw, bias):
            q = q_ref[hh, :, pl.ds(t0 - t_begin, QB)]
            g = g_ref[hh]
            s = jnp.dot(kw, q, preferred_element_type=jnp.float32) * inv_scale
            if bias is not None:
                s = s + bias
            s = jnp.where(win_keep, s, neg)
            top = jnp.max(s, axis=0, keepdims=True)
            p = jnp.exp(s - top)
            total = jnp.sum(p, axis=0, keepdims=True)
            window = jnp.dot(vw, p.astype(jnp.bfloat16), preferred_element_type=jnp.float32)
            window = window * (1.0 / total)

            logits = jnp.dot(fq_ref[hh], q, preferred_element_type=jnp.float32)
            m_lo = jnp.max(logits[:half], axis=0, keepdims=True)
            m_hi = jnp.max(logits[half:], axis=0, keepdims=True)
            e = jnp.exp(logits - jnp.where(lo, m_lo, m_hi))
            s_lo = jnp.sum(e[:half], axis=0, keepdims=True)
            s_hi = jnp.sum(e[half:], axis=0, keepdims=True)
            phi = (e * jnp.where(lo, 1.0 / s_lo, 1.0 / s_hi)).astype(jnp.bfloat16)

            aff = jnp.dot(pkw, phi, preferred_element_type=jnp.float32)
            aff = jnp.where(lin_keep, aff, jnp.float32(0.0)).astype(jnp.bfloat16)
            num = jnp.dot(vw, aff, preferred_element_type=jnp.float32)
            den = jnp.sum(aff.astype(jnp.float32), axis=0, keepdims=True)
            st_hi = st.astype(jnp.bfloat16)
            st_lo = (st - st_hi.astype(jnp.float32)).astype(jnp.bfloat16)
            num = num + jnp.dot(st_hi, phi, preferred_element_type=jnp.float32)
            num = num + jnp.dot(st_lo, phi, preferred_element_type=jnp.float32)
            z_hi = z.astype(jnp.bfloat16)
            z_lo = (z - z_hi.astype(jnp.float32)).astype(jnp.bfloat16)
            zz = jnp.where(zrow == 0, z_hi, jnp.where(zrow == 1, z_lo, jnp.zeros_like(z_lo)))
            cross = jnp.dot(zz, phi, preferred_element_type=jnp.float32)
            den = den + (cross[0:1] + cross[1:2])
            linear = num * (1.0 / (den + 1.0))
            out = g * window + (1.0 - g) * linear
            rows = pl.ds(t0 - t_begin, QB)
            o_ref[rows, pl.ds(hh * head_dim, head_dim)] = out.T.astype(o_ref.dtype)

            vb = vw[:, :QB]
            pkb = pkw[:QB]
            st = st + jnp.dot(vb, pkb, preferred_element_type=jnp.float32)
            z = z + jnp.sum(pkb.astype(jnp.float32), axis=0, keepdims=True)
            return st, z

        carry = []
        for hh in range(heads):
            if first:
                kw0 = jnp.concatenate([kh_ref[hh], k_ref[hh, pl.ds(0, QB), :]], axis=0)
                vw0 = jnp.concatenate([vh_ref[hh], v_ref[hh, :, pl.ds(0, QB)]], axis=1)
                pkw0 = jnp.concatenate([pkh_ref[hh], pk_ref[hh, pl.ds(0, QB), :]], axis=0)
                carry.append(step(hh, 0, st_ref[hh], z_ref[hh][0:1], kw0, vw0, pkw0, b_ref[...]))
            else:
                carry.append((st_ref[hh], z_ref[hh][0:1]))

        def one(t0, carry):
            base = t0 - QB
            out = []
            for hh in range(heads):
                kw = k_ref[hh, pl.ds(base, 2 * QB), :]
                vw = v_ref[hh, :, pl.ds(base, 2 * QB)]
                pkw = pk_ref[hh, pl.ds(base, 2 * QB), :]
                out.append(step(hh, t0, carry[hh][0], carry[hh][1], kw, vw, pkw, None))
            return tuple(out)

        lo_blk = t_begin // QB + (1 if first else 0)
        hi_blk = t_begin // QB + blocks
        pairs = (hi_blk - lo_blk) // UNROLL

        def loop(i, carry):
            for u in range(UNROLL):
                t0 = pl.multiple_of((lo_blk + i * UNROLL + u) * QB, QB)
                carry = one(t0, carry)
            return carry

        final = lax.fori_loop(0, pairs, loop, tuple(carry))
        for blk in range(lo_blk + pairs * UNROLL, hi_blk):
            final = one(blk * QB, final)
        if first:
            for hh in range(heads):
                st_out[hh] = final[hh][0]
                z_out[hh] = jnp.broadcast_to(final[hh][1], (8, feats))

    return attend_kernel


def attend(q, t_begin, k_tm, v, pk, kh, vh, pkh, fq_t, st0, z0, gate_rows, bias0, prev):
    group, head_dim, span = q.shape
    length = v.shape[2]
    feats = fq_t.shape[1]
    hb = HEADS_PER_STEP
    first = prev is None
    in_specs = [
        pl.BlockSpec((hb, head_dim, span), lambda h: (h, 0, 0)),
        pl.BlockSpec((hb, length, head_dim), lambda h: (h, 0, 0)),
        pl.BlockSpec((hb, head_dim, length), lambda h: (h, 0, 0)),
        pl.BlockSpec((hb, length, feats), lambda h: (h, 0, 0)),
        pl.BlockSpec((hb, QB, head_dim), lambda h: (h, 0, 0)),
        pl.BlockSpec((hb, head_dim, QB), lambda h: (h, 0, 0)),
        pl.BlockSpec((hb, QB, feats), lambda h: (h, 0, 0)),
        pl.BlockSpec((hb, feats, head_dim), lambda h: (h, 0, 0)),
        pl.BlockSpec((hb, head_dim, feats), lambda h: (h, 0, 0)),
        pl.BlockSpec((hb, 8, feats), lambda h: (h, 0, 0)),
        pl.BlockSpec((hb, 1, QB), lambda h: (h, 0, 0)),
        pl.BlockSpec((2 * QB, QB), lambda h: (0, 0)),
    ]
    args = [q, k_tm, v, pk, kh, vh, pkh, fq_t, st0, z0, gate_rows, bias0]
    piece = t_begin // span
    out_spec = pl.BlockSpec((span, hb * head_dim), lambda h: (piece, h))
    out_shape = jax.ShapeDtypeStruct((length, group * head_dim), jnp.bfloat16)
    if first:
        out_specs = [
            out_spec,
            pl.BlockSpec((hb, head_dim, feats), lambda h: (h, 0, 0)),
            pl.BlockSpec((hb, 8, feats), lambda h: (h, 0, 0)),
        ]
        out_shapes = [
            out_shape,
            jax.ShapeDtypeStruct(st0.shape, jnp.float32),
            jax.ShapeDtypeStruct(z0.shape, jnp.float32),
        ]
        aliases = {}
    else:
        in_specs.append(pl.BlockSpec(memory_space=pl.ANY))
        args.append(prev)
        out_specs = out_spec
        out_shapes = out_shape
        aliases = {12: 0}
    return pl.pallas_call(
        make_kernel(t_begin, span // QB),
        grid=(group // hb,),
        in_specs=in_specs,
        out_specs=out_specs,
        out_shape=out_shapes,
        input_output_aliases=aliases,
        interpret=INTERPRET,
    )(*args)


def local_part(q_parts, k, v, before, earlier, feat_q, feat_k, prior_state, prior_norm, gate):
    group, head_dim, length = k.shape
    keep = earlier.astype(jnp.bfloat16)
    phi_k = feature_map(k, feat_k)
    phi_halo = feature_map(before[0], feat_k) * keep
    halo_state = jnp.einsum(
        "htf,hdt->hdf", phi_halo, before[1], preferred_element_type=jnp.float32
    )
    halo_norm = jnp.sum(phi_halo, axis=1, dtype=jnp.float32)
    feats = phi_k.shape[2]
    pad_k = jnp.zeros((group, head_dim, QB - WIN), k.dtype)
    kh = jnp.concatenate([pad_k, before[0]], axis=2).transpose(0, 2, 1)
    vh = jnp.concatenate([pad_k, before[1]], axis=2)
    pkh = jnp.concatenate([jnp.zeros((group, QB - WIN, feats), phi_k.dtype), phi_halo], axis=1)
    fq_t = jnp.concatenate([feat_q, -feat_q], axis=2).transpose(0, 2, 1)
    st = prior_state - halo_state
    z = jnp.pad((prior_norm - halo_norm)[:, None, :], ((0, 0), (0, 7), (0, 0)))
    gate_rows = jnp.broadcast_to(gate[:, None, None], (group, 1, QB)).astype(jnp.float32)
    halo_rows = (jnp.arange(2 * QB) >= QB - WIN) & (jnp.arange(2 * QB) < QB)
    bias0 = jnp.where(halo_rows & jnp.logical_not(earlier), jnp.float32(-1e30), jnp.float32(0.0))
    bias0 = jnp.broadcast_to(bias0[:, None], (2 * QB, QB))
    k_tm = k.transpose(0, 2, 1)
    span = q_parts[0].shape[2]
    out, st, z = attend(q_parts[0], 0, k_tm, v, phi_k, kh, vh, pkh, fq_t, st, z, gate_rows, bias0, None)
    for c in range(1, len(q_parts)):
        out = attend(q_parts[c], c * span, k_tm, v, phi_k, kh, vh, pkh, fq_t, st, z, gate_rows, bias0, out)
    return out


def body(queries, keys, values, feat_q, feat_k, mix):
    shards = lax.axis_size("seq")
    place = lax.axis_index("seq")
    feature_rows = queries.shape[0]
    length = queries.shape[1] // shards
    group = feat_q.shape[0]
    head_dim = feat_q.shape[1]

    halves = queries.reshape(feature_rows, shards, Q_PIECES, length // Q_PIECES).transpose(2, 1, 0, 3)
    halves, values = lax.optimization_barrier((halves, values))
    k = exchange(keys.reshape(feature_rows, shards, length), group, head_dim)
    v = exchange(values.reshape(feature_rows, shards, length), group, head_dim)
    q_parts = [
        lax.all_to_all(halves[c], "seq", split_axis=0, concat_axis=0, tiled=True).reshape(
            group, head_dim, -1
        )
        for c in range(Q_PIECES)
    ]

    earlier = place > 0
    tails = jnp.stack([k[:, :, length - WIN :], v[:, :, length - WIN :]])
    before = passed_along(tails, "seq", 1)

    phi_own = feature_map(k, feat_k)
    own_state = jnp.einsum("htf,hdt->hdf", phi_own, v, preferred_element_type=jnp.float32)
    own_norm = jnp.sum(phi_own, axis=1, dtype=jnp.float32)
    own = jnp.concatenate([own_state.reshape(group * head_dim, -1), own_norm], axis=0)
    prior = own
    distance = 1
    while distance < shards:
        prior = prior + passed_along(prior.astype(jnp.bfloat16), "seq", distance).astype(jnp.float32)
        distance *= 2
    prior = prior - own
    prior_state = prior[: group * head_dim].reshape(own_state.shape)
    prior_norm = prior[group * head_dim :]
    gate = jax.nn.sigmoid(mix)
    return local_part(q_parts, k, v, before, earlier, feat_q, feat_k, prior_state, prior_norm, gate)


def solution(mesh):
    return jax.shard_map(
        body,
        mesh=mesh,
        in_specs=(
            P(("heads", "seq"), None),
            P(("heads", "seq"), None),
            P(("heads", "seq"), None),
            P("heads", None, None),
            P("heads", None, None),
            P("heads"),
        ),
        out_specs=P("seq", "heads"),
        check_vma=False,
    )
```

```python
import functools

import jax
import jax.numpy as jnp
from jax import lax
from jax.experimental import pallas as pl
from jax.experimental.pallas import tpu as pltpu
from jax.sharding import PartitionSpec as P

WIN = 64
QB = 128
HEADS_PER_STEP = 2
Q_PIECES = 2
UNROLL = 8
RADIX = 4
INTERPRET = False


def passed_along(block, axis, distance):
    devices = range(lax.axis_size(axis))
    route = [(i - distance, i) for i in devices if i - distance in devices]
    return lax.ppermute(block, axis, route)


def exchange(rows, group, head_dim):
    moved = lax.all_to_all(rows, "seq", split_axis=1, concat_axis=0, tiled=True)
    return moved.reshape(group, head_dim, -1)


def feature_map(rows, weight):
    logits = jnp.einsum("hdt,hdf->htf", rows, weight, preferred_element_type=jnp.float32)
    halves = [jax.nn.softmax(logits, axis=-1), jax.nn.softmax(-logits, axis=-1)]
    return jnp.concatenate(halves, axis=-1).astype(jnp.bfloat16)


def _nt(a, b):
    return lax.dot_general(a, b, (((1,), (1,)), ((), ())), preferred_element_type=jnp.float32)


def _tn(a, b):
    return lax.dot_general(a, b, (((0,), (0,)), ((), ())), preferred_element_type=jnp.float32)


def make_kernel(t_begin, blocks):
    first = t_begin == 0

    def attend_kernel(*refs):
        (q_ref, k_ref, v_ref, pk_ref, kh_ref, vh_ref, pkh_ref, fq_ref, st_ref, z_ref, g_ref, b_ref) = refs[:12]
        if first:
            o_ref, st_out, z_out = refs[12:]
        else:
            o_ref = refs[13]
        heads = q_ref.shape[0]
        head_dim = q_ref.shape[1]
        feats = fq_ref.shape[1]
        half = feats // 2
        inv_scale = 1.0 / jnp.sqrt(jnp.float32(head_dim))
        row = lax.broadcasted_iota(jnp.int32, (feats, QB), 0)
        lo = row < half
        wk = lax.broadcasted_iota(jnp.int32, (2 * QB, QB), 0)
        tq = lax.broadcasted_iota(jnp.int32, (2 * QB, QB), 1)
        win_keep = (wk > tq + WIN) & (wk <= tq + QB)
        lin_keep = wk <= tq + WIN
        zrow = lax.broadcasted_iota(jnp.int32, (8, feats), 0)
        neg = jnp.float32(-1e30)

        def step(hh, t0, st, z, kw, vw, pkw, bias):
            q = q_ref[hh, :, pl.ds(t0 - t_begin, QB)]
            g = g_ref[hh]
            s = jnp.dot(kw, q, preferred_element_type=jnp.float32) * inv_scale
            if bias is not None:
                s = s + bias
            s = jnp.where(win_keep, s, neg)
            top = jnp.max(s, axis=0, keepdims=True)
            p = jnp.exp(s - top)
            total = jnp.sum(p, axis=0, keepdims=True)
            window = jnp.dot(vw, p.astype(jnp.bfloat16), preferred_element_type=jnp.float32)
            window = window * (1.0 / total)

            logits = jnp.dot(fq_ref[hh], q, preferred_element_type=jnp.float32)
            m_lo = jnp.max(logits[:half], axis=0, keepdims=True)
            m_hi = jnp.max(logits[half:], axis=0, keepdims=True)
            e = jnp.exp(logits - jnp.where(lo, m_lo, m_hi))
            s_lo = jnp.sum(e[:half], axis=0, keepdims=True)
            s_hi = jnp.sum(e[half:], axis=0, keepdims=True)
            phi = (e * jnp.where(lo, 1.0 / s_lo, 1.0 / s_hi)).astype(jnp.bfloat16)

            aff = jnp.dot(pkw, phi, preferred_element_type=jnp.float32)
            aff = jnp.where(lin_keep, aff, jnp.float32(0.0)).astype(jnp.bfloat16)
            num = jnp.dot(vw, aff, preferred_element_type=jnp.float32)
            den = jnp.sum(aff.astype(jnp.float32), axis=0, keepdims=True)
            st_hi = st.astype(jnp.bfloat16)
            st_lo = (st - st_hi.astype(jnp.float32)).astype(jnp.bfloat16)
            num = num + jnp.dot(st_hi, phi, preferred_element_type=jnp.float32)
            num = num + jnp.dot(st_lo, phi, preferred_element_type=jnp.float32)
            z_hi = z.astype(jnp.bfloat16)
            z_lo = (z - z_hi.astype(jnp.float32)).astype(jnp.bfloat16)
            zz = jnp.where(zrow == 0, z_hi, jnp.where(zrow == 1, z_lo, jnp.zeros_like(z_lo)))
            cross = jnp.dot(zz, phi, preferred_element_type=jnp.float32)
            den = den + (cross[0:1] + cross[1:2])
            linear = num * (1.0 / (den + 1.0))
            out = g * window + (1.0 - g) * linear
            rows = pl.ds(t0 - t_begin, QB)
            o_ref[rows, pl.ds(hh * head_dim, head_dim)] = out.T.astype(o_ref.dtype)

            vb = vw[:, :QB]
            pkb = pkw[:QB]
            st = st + jnp.dot(vb, pkb, preferred_element_type=jnp.float32)
            z = z + jnp.sum(pkb.astype(jnp.float32), axis=0, keepdims=True)
            return st, z

        carry = []
        for hh in range(heads):
            if first:
                kw0 = jnp.concatenate([kh_ref[hh], k_ref[hh, pl.ds(0, QB), :]], axis=0)
                vw0 = jnp.concatenate([vh_ref[hh], v_ref[hh, :, pl.ds(0, QB)]], axis=1)
                pkw0 = jnp.concatenate([pkh_ref[hh], pk_ref[hh, pl.ds(0, QB), :]], axis=0)
                carry.append(step(hh, 0, st_ref[hh], z_ref[hh][0:1], kw0, vw0, pkw0, b_ref[...]))
            else:
                carry.append((st_ref[hh], z_ref[hh][0:1]))

        def one(t0, carry):
            base = t0 - QB
            out = []
            for hh in range(heads):
                kw = k_ref[hh, pl.ds(base, 2 * QB), :]
                vw = v_ref[hh, :, pl.ds(base, 2 * QB)]
                pkw = pk_ref[hh, pl.ds(base, 2 * QB), :]
                out.append(step(hh, t0, carry[hh][0], carry[hh][1], kw, vw, pkw, None))
            return tuple(out)

        lo_blk = t_begin // QB + (1 if first else 0)
        hi_blk = t_begin // QB + blocks
        pairs = (hi_blk - lo_blk) // UNROLL

        def loop(i, carry):
            for u in range(UNROLL):
                t0 = pl.multiple_of((lo_blk + i * UNROLL + u) * QB, QB)
                carry = one(t0, carry)
            return carry

        final = lax.fori_loop(0, pairs, loop, tuple(carry))
        for blk in range(lo_blk + pairs * UNROLL, hi_blk):
            final = one(blk * QB, final)
        if first:
            for hh in range(heads):
                st_out[hh] = final[hh][0]
                z_out[hh] = jnp.broadcast_to(final[hh][1], (8, feats))

    return attend_kernel


def attend(q, t_begin, k_tm, v, pk, kh, vh, pkh, fq_t, st0, z0, gate_rows, bias0, prev):
    group, head_dim, span = q.shape
    length = v.shape[2]
    feats = fq_t.shape[1]
    hb = HEADS_PER_STEP
    first = prev is None
    in_specs = [
        pl.BlockSpec((hb, head_dim, span), lambda h: (h, 0, 0)),
        pl.BlockSpec((hb, length, head_dim), lambda h: (h, 0, 0)),
        pl.BlockSpec((hb, head_dim, length), lambda h: (h, 0, 0)),
        pl.BlockSpec((hb, length, feats), lambda h: (h, 0, 0)),
        pl.BlockSpec((hb, QB, head_dim), lambda h: (h, 0, 0)),
        pl.BlockSpec((hb, head_dim, QB), lambda h: (h, 0, 0)),
        pl.BlockSpec((hb, QB, feats), lambda h: (h, 0, 0)),
        pl.BlockSpec((hb, feats, head_dim), lambda h: (h, 0, 0)),
        pl.BlockSpec((hb, head_dim, feats), lambda h: (h, 0, 0)),
        pl.BlockSpec((hb, 8, feats), lambda h: (h, 0, 0)),
        pl.BlockSpec((hb, 1, QB), lambda h: (h, 0, 0)),
        pl.BlockSpec((2 * QB, QB), lambda h: (0, 0)),
    ]
    args = [q, k_tm, v, pk, kh, vh, pkh, fq_t, st0, z0, gate_rows, bias0]
    piece = t_begin // span
    out_spec = pl.BlockSpec((span, hb * head_dim), lambda h: (piece, h))
    out_shape = jax.ShapeDtypeStruct((length, group * head_dim), jnp.bfloat16)
    if first:
        out_specs = [
            out_spec,
            pl.BlockSpec((hb, head_dim, feats), lambda h: (h, 0, 0)),
            pl.BlockSpec((hb, 8, feats), lambda h: (h, 0, 0)),
        ]
        out_shapes = [
            out_shape,
            jax.ShapeDtypeStruct(st0.shape, jnp.float32),
            jax.ShapeDtypeStruct(z0.shape, jnp.float32),
        ]
        aliases = {}
    else:
        in_specs.append(pl.BlockSpec(memory_space=pl.ANY))
        args.append(prev)
        out_specs = out_spec
        out_shapes = out_shape
        aliases = {12: 0}
    return pl.pallas_call(
        make_kernel(t_begin, span // QB),
        grid=(group // hb,),
        in_specs=in_specs,
        out_specs=out_specs,
        out_shape=out_shapes,
        input_output_aliases=aliases,
        interpret=INTERPRET,
    )(*args)


def local_part(q_parts, k, v, before, earlier, feat_q, feat_k, prior_state, prior_norm, gate):
    group, head_dim, length = k.shape
    keep = earlier.astype(jnp.bfloat16)
    phi_k = feature_map(k, feat_k)
    phi_halo = feature_map(before[0], feat_k) * keep
    halo_state = jnp.einsum(
        "htf,hdt->hdf", phi_halo, before[1], preferred_element_type=jnp.float32
    )
    halo_norm = jnp.sum(phi_halo, axis=1, dtype=jnp.float32)
    feats = phi_k.shape[2]
    pad_k = jnp.zeros((group, head_dim, QB - WIN), k.dtype)
    kh = jnp.concatenate([pad_k, before[0]], axis=2).transpose(0, 2, 1)
    vh = jnp.concatenate([pad_k, before[1]], axis=2)
    pkh = jnp.concatenate([jnp.zeros((group, QB - WIN, feats), phi_k.dtype), phi_halo], axis=1)
    fq_t = jnp.concatenate([feat_q, -feat_q], axis=2).transpose(0, 2, 1)
    st = prior_state - halo_state
    z = jnp.pad((prior_norm - halo_norm)[:, None, :], ((0, 0), (0, 7), (0, 0)))
    gate_rows = jnp.broadcast_to(gate[:, None, None], (group, 1, QB)).astype(jnp.float32)
    halo_rows = (jnp.arange(2 * QB) >= QB - WIN) & (jnp.arange(2 * QB) < QB)
    bias0 = jnp.where(halo_rows & jnp.logical_not(earlier), jnp.float32(-1e30), jnp.float32(0.0))
    bias0 = jnp.broadcast_to(bias0[:, None], (2 * QB, QB))
    k_tm = k.transpose(0, 2, 1)
    span = q_parts[0].shape[2]
    out, st, z = attend(q_parts[0], 0, k_tm, v, phi_k, kh, vh, pkh, fq_t, st, z, gate_rows, bias0, None)
    for c in range(1, len(q_parts)):
        out = attend(q_parts[c], c * span, k_tm, v, phi_k, kh, vh, pkh, fq_t, st, z, gate_rows, bias0, out)
    return out


def body(queries, keys, values, feat_q, feat_k, mix):
    shards = lax.axis_size("seq")
    place = lax.axis_index("seq")
    feature_rows = queries.shape[0]
    length = queries.shape[1] // shards
    group = feat_q.shape[0]
    head_dim = feat_q.shape[1]

    halves = queries.reshape(feature_rows, shards, Q_PIECES, length // Q_PIECES).transpose(2, 1, 0, 3)
    halves, values = lax.optimization_barrier((halves, values))
    k = exchange(keys.reshape(feature_rows, shards, length), group, head_dim)
    v = exchange(values.reshape(feature_rows, shards, length), group, head_dim)
    q_parts = [
        lax.all_to_all(halves[c], "seq", split_axis=0, concat_axis=0, tiled=True).reshape(
            group, head_dim, -1
        )
        for c in range(Q_PIECES)
    ]

    earlier = place > 0
    tails = jnp.stack([k[:, :, length - WIN :], v[:, :, length - WIN :]])
    before = passed_along(tails, "seq", 1)

    phi_own = feature_map(k, feat_k)
    own_state = jnp.einsum("htf,hdt->hdf", phi_own, v, preferred_element_type=jnp.float32)
    own_norm = jnp.sum(phi_own, axis=1, dtype=jnp.float32)
    own = jnp.concatenate([own_state.reshape(group * head_dim, -1), own_norm], axis=0)
    prior = own
    distance = 1
    while distance < shards:
        sent = prior.astype(jnp.bfloat16)
        total = prior
        for j in range(1, RADIX):
            if distance * j < shards:
                total = total + passed_along(sent, "seq", distance * j).astype(jnp.float32)
        prior = total
        distance *= RADIX
    prior = prior - own
    prior_state = prior[: group * head_dim].reshape(own_state.shape)
    prior_norm = prior[group * head_dim :]
    gate = jax.nn.sigmoid(mix)
    return local_part(q_parts, k, v, before, earlier, feat_q, feat_k, prior_state, prior_norm, gate)


def solution(mesh):
    return jax.shard_map(
        body,
        mesh=mesh,
        in_specs=(
            P(("heads", "seq"), None),
            P(("heads", "seq"), None),
            P(("heads", "seq"), None),
            P("heads", None, None),
            P("heads", None, None),
            P("heads"),
        ),
        out_specs=P("seq", "heads"),
        check_vma=False,
    )
```

```python
import functools

import jax
import jax.numpy as jnp
from jax import lax
from jax.experimental import pallas as pl
from jax.experimental.pallas import tpu as pltpu
from jax.sharding import PartitionSpec as P

WIN = 64
QB = 128
HEADS_PER_STEP = 2
Q_PIECES = 2
UNROLL = 8
RADIX = 4
INTERPRET = False


def passed_along(block, axis, distance):
    devices = range(lax.axis_size(axis))
    route = [(i - distance, i) for i in devices if i - distance in devices]
    return lax.ppermute(block, axis, route)


def exchange(rows, group, head_dim):
    moved = lax.all_to_all(rows, "seq", split_axis=1, concat_axis=0, tiled=True)
    return moved.reshape(group, head_dim, -1)


def feature_map(rows, weight):
    logits = jnp.einsum("hdt,hdf->htf", rows, weight, preferred_element_type=jnp.float32)
    halves = [jax.nn.softmax(logits, axis=-1), jax.nn.softmax(-logits, axis=-1)]
    return jnp.concatenate(halves, axis=-1).astype(jnp.bfloat16)


def _nt(a, b):
    return lax.dot_general(a, b, (((1,), (1,)), ((), ())), preferred_element_type=jnp.float32)


def _tn(a, b):
    return lax.dot_general(a, b, (((0,), (0,)), ((), ())), preferred_element_type=jnp.float32)


def make_kernel(t_begin, blocks):
    first = t_begin == 0

    def attend_kernel(*refs):
        (q_ref, k_ref, v_ref, pk_ref, kh_ref, vh_ref, pkh_ref, fq_ref, st_ref, z_ref, g_ref, b_ref) = refs[:12]
        if first:
            o_ref, st_out, z_out = refs[12:]
        else:
            o_ref = refs[13]
        heads = q_ref.shape[0]
        head_dim = q_ref.shape[1]
        feats = fq_ref.shape[1]
        half = feats // 2
        inv_scale = 1.0 / jnp.sqrt(jnp.float32(head_dim))
        row = lax.broadcasted_iota(jnp.int32, (feats, QB), 0)
        lo = row < half
        wk = lax.broadcasted_iota(jnp.int32, (2 * QB, QB), 0)
        tq = lax.broadcasted_iota(jnp.int32, (2 * QB, QB), 1)
        win_keep = (wk > tq + WIN) & (wk <= tq + QB)
        lin_keep = wk <= tq + WIN
        zrow = lax.broadcasted_iota(jnp.int32, (8, feats), 0)
        neg = jnp.float32(-1e30)

        def step(hh, t0, st, z, kw, vw, pkw, bias):
            q = q_ref[hh, :, pl.ds(t0 - t_begin, QB)]
            g = g_ref[hh]
            s = jnp.dot(kw, q, preferred_element_type=jnp.float32) * inv_scale
            if bias is not None:
                s = s + bias
            s = jnp.where(win_keep, s, neg)
            top = jnp.max(s, axis=0, keepdims=True)
            p = jnp.exp(s - top)
            total = jnp.sum(p, axis=0, keepdims=True)
            window = jnp.dot(vw, p.astype(jnp.bfloat16), preferred_element_type=jnp.float32)
            window = window * (1.0 / total)

            logits = jnp.dot(fq_ref[hh], q, preferred_element_type=jnp.float32)
            m_lo = jnp.max(logits[:half], axis=0, keepdims=True)
            m_hi = jnp.max(logits[half:], axis=0, keepdims=True)
            e = jnp.exp(logits - jnp.where(lo, m_lo, m_hi))
            s_lo = jnp.sum(e[:half], axis=0, keepdims=True)
            s_hi = jnp.sum(e[half:], axis=0, keepdims=True)
            phi = (e * jnp.where(lo, 1.0 / s_lo, 1.0 / s_hi)).astype(jnp.bfloat16)

            aff = jnp.dot(pkw, phi, preferred_element_type=jnp.float32)
            aff = jnp.where(lin_keep, aff, jnp.float32(0.0)).astype(jnp.bfloat16)
            num = jnp.dot(vw, aff, preferred_element_type=jnp.float32)
            den = jnp.sum(aff.astype(jnp.float32), axis=0, keepdims=True)
            st_hi = st.astype(jnp.bfloat16)
            st_lo = (st - st_hi.astype(jnp.float32)).astype(jnp.bfloat16)
            num = num + jnp.dot(st_hi, phi, preferred_element_type=jnp.float32)
            num = num + jnp.dot(st_lo, phi, preferred_element_type=jnp.float32)
            z_hi = z.astype(jnp.bfloat16)
            z_lo = (z - z_hi.astype(jnp.float32)).astype(jnp.bfloat16)
            zz = jnp.where(zrow == 0, z_hi, jnp.where(zrow == 1, z_lo, jnp.zeros_like(z_lo)))
            cross = jnp.dot(zz, phi, preferred_element_type=jnp.float32)
            den = den + (cross[0:1] + cross[1:2])
            linear = num * (1.0 / (den + 1.0))
            out = g * window + (1.0 - g) * linear
            rows = pl.ds(t0 - t_begin, QB)
            o_ref[rows, pl.ds(hh * head_dim, head_dim)] = out.T.astype(o_ref.dtype)

            vb = vw[:, :QB]
            pkb = pkw[:QB]
            st = st + jnp.dot(vb, pkb, preferred_element_type=jnp.float32)
            z = z + jnp.sum(pkb.astype(jnp.float32), axis=0, keepdims=True)
            return st, z

        carry = []
        for hh in range(heads):
            if first:
                kw0 = jnp.concatenate([kh_ref[hh], k_ref[hh, pl.ds(0, QB), :]], axis=0)
                vw0 = jnp.concatenate([vh_ref[hh], v_ref[hh, :, pl.ds(0, QB)]], axis=1)
                pkw0 = jnp.concatenate([pkh_ref[hh], pk_ref[hh, pl.ds(0, QB), :]], axis=0)
                carry.append(step(hh, 0, st_ref[hh], z_ref[hh][0:1], kw0, vw0, pkw0, b_ref[...]))
            else:
                carry.append((st_ref[hh], z_ref[hh][0:1]))

        def one(t0, carry):
            base = t0 - QB
            out = []
            for hh in range(heads):
                kw = k_ref[hh, pl.ds(base, 2 * QB), :]
                vw = v_ref[hh, :, pl.ds(base, 2 * QB)]
                pkw = pk_ref[hh, pl.ds(base, 2 * QB), :]
                out.append(step(hh, t0, carry[hh][0], carry[hh][1], kw, vw, pkw, None))
            return tuple(out)

        lo_blk = t_begin // QB + (1 if first else 0)
        hi_blk = t_begin // QB + blocks
        pairs = (hi_blk - lo_blk) // UNROLL

        def loop(i, carry):
            for u in range(UNROLL):
                t0 = pl.multiple_of((lo_blk + i * UNROLL + u) * QB, QB)
                carry = one(t0, carry)
            return carry

        final = lax.fori_loop(0, pairs, loop, tuple(carry))
        for blk in range(lo_blk + pairs * UNROLL, hi_blk):
            final = one(blk * QB, final)
        if first:
            for hh in range(heads):
                st_out[hh] = final[hh][0]
                z_out[hh] = jnp.broadcast_to(final[hh][1], (8, feats))

    return attend_kernel


def attend(q, t_begin, k_tm, v, pk, kh, vh, pkh, fq_t, st0, z0, gate_rows, bias0, prev):
    group, head_dim, span = q.shape
    length = v.shape[2]
    feats = fq_t.shape[1]
    hb = HEADS_PER_STEP
    first = prev is None
    in_specs = [
        pl.BlockSpec((hb, head_dim, span), lambda h: (h, 0, 0)),
        pl.BlockSpec((hb, length, head_dim), lambda h: (h, 0, 0)),
        pl.BlockSpec((hb, head_dim, length), lambda h: (h, 0, 0)),
        pl.BlockSpec((hb, length, feats), lambda h: (h, 0, 0)),
        pl.BlockSpec((hb, QB, head_dim), lambda h: (h, 0, 0)),
        pl.BlockSpec((hb, head_dim, QB), lambda h: (h, 0, 0)),
        pl.BlockSpec((hb, QB, feats), lambda h: (h, 0, 0)),
        pl.BlockSpec((hb, feats, head_dim), lambda h: (h, 0, 0)),
        pl.BlockSpec((hb, head_dim, feats), lambda h: (h, 0, 0)),
        pl.BlockSpec((hb, 8, feats), lambda h: (h, 0, 0)),
        pl.BlockSpec((hb, 1, QB), lambda h: (h, 0, 0)),
        pl.BlockSpec((2 * QB, QB), lambda h: (0, 0)),
    ]
    args = [q, k_tm, v, pk, kh, vh, pkh, fq_t, st0, z0, gate_rows, bias0]
    piece = t_begin // span
    out_spec = pl.BlockSpec((span, hb * head_dim), lambda h: (piece, h))
    out_shape = jax.ShapeDtypeStruct((length, group * head_dim), jnp.bfloat16)
    if first:
        out_specs = [
            out_spec,
            pl.BlockSpec((hb, head_dim, feats), lambda h: (h, 0, 0)),
            pl.BlockSpec((hb, 8, feats), lambda h: (h, 0, 0)),
        ]
        out_shapes = [
            out_shape,
            jax.ShapeDtypeStruct(st0.shape, jnp.float32),
            jax.ShapeDtypeStruct(z0.shape, jnp.float32),
        ]
        aliases = {}
    else:
        in_specs.append(pl.BlockSpec(memory_space=pl.ANY))
        args.append(prev)
        out_specs = out_spec
        out_shapes = out_shape
        aliases = {12: 0}
    return pl.pallas_call(
        make_kernel(t_begin, span // QB),
        grid=(group // hb,),
        in_specs=in_specs,
        out_specs=out_specs,
        out_shape=out_shapes,
        input_output_aliases=aliases,
        interpret=INTERPRET,
    )(*args)


def local_part(q_parts, k, v, before, earlier, feat_q, feat_k, prior_state, prior_norm, gate):
    group, head_dim, length = k.shape
    keep = earlier.astype(jnp.bfloat16)
    phi_k = feature_map(k, feat_k)
    phi_halo = feature_map(before[0], feat_k) * keep
    halo_state = jnp.einsum(
        "htf,hdt->hdf", phi_halo, before[1], preferred_element_type=jnp.float32
    )
    halo_norm = jnp.sum(phi_halo, axis=1, dtype=jnp.float32)
    feats = phi_k.shape[2]
    pad_k = jnp.zeros((group, head_dim, QB - WIN), k.dtype)
    kh = jnp.concatenate([pad_k, before[0]], axis=2).transpose(0, 2, 1)
    vh = jnp.concatenate([pad_k, before[1]], axis=2)
    pkh = jnp.concatenate([jnp.zeros((group, QB - WIN, feats), phi_k.dtype), phi_halo], axis=1)
    fq_t = jnp.concatenate([feat_q, -feat_q], axis=2).transpose(0, 2, 1)
    st = prior_state - halo_state
    z = jnp.pad((prior_norm - halo_norm)[:, None, :], ((0, 0), (0, 7), (0, 0)))
    gate_rows = jnp.broadcast_to(gate[:, None, None], (group, 1, QB)).astype(jnp.float32)
    halo_rows = (jnp.arange(2 * QB) >= QB - WIN) & (jnp.arange(2 * QB) < QB)
    bias0 = jnp.where(halo_rows & jnp.logical_not(earlier), jnp.float32(-1e30), jnp.float32(0.0))
    bias0 = jnp.broadcast_to(bias0[:, None], (2 * QB, QB))
    k_tm = k.transpose(0, 2, 1)
    span = q_parts[0].shape[2]
    out, st, z = attend(q_parts[0], 0, k_tm, v, phi_k, kh, vh, pkh, fq_t, st, z, gate_rows, bias0, None)
    for c in range(1, len(q_parts)):
        out = attend(q_parts[c], c * span, k_tm, v, phi_k, kh, vh, pkh, fq_t, st, z, gate_rows, bias0, out)
    return out


def body(queries, keys, values, feat_q, feat_k, mix):
    shards = lax.axis_size("seq")
    place = lax.axis_index("seq")
    feature_rows = queries.shape[0]
    length = queries.shape[1] // shards
    group = feat_q.shape[0]
    head_dim = feat_q.shape[1]

    halves = queries.reshape(feature_rows, shards, Q_PIECES, length // Q_PIECES).transpose(2, 1, 0, 3)
    halves, values = lax.optimization_barrier((halves, values))
    k = exchange(keys.reshape(feature_rows, shards, length), group, head_dim)
    v = exchange(values.reshape(feature_rows, shards, length), group, head_dim)
    q_parts = [
        lax.all_to_all(halves[c], "seq", split_axis=0, concat_axis=0, tiled=True).reshape(
            group, head_dim, -1
        )
        for c in range(Q_PIECES - 1)
    ]
    late_q = halves[Q_PIECES - 1]

    earlier = place > 0
    tails = jnp.stack([k[:, :, length - WIN :], v[:, :, length - WIN :]])
    before = passed_along(tails, "seq", 1)

    phi_own = feature_map(k, feat_k)
    own_state = jnp.einsum("htf,hdt->hdf", phi_own, v, preferred_element_type=jnp.float32)
    own_norm = jnp.sum(phi_own, axis=1, dtype=jnp.float32)
    own = jnp.concatenate([own_state.reshape(group * head_dim, -1), own_norm], axis=0)
    prior = own
    distance = 1
    while distance < shards:
        sent = prior.astype(jnp.bfloat16)
        total = prior
        for j in range(1, RADIX):
            if distance * j < shards:
                total = total + passed_along(sent, "seq", distance * j).astype(jnp.float32)
        prior = total
        if distance == 1:
            late_q, prior = lax.optimization_barrier((late_q, prior))
        distance *= RADIX
    prior = prior - own
    q_parts.append(
        lax.all_to_all(late_q, "seq", split_axis=0, concat_axis=0, tiled=True).reshape(
            group, head_dim, -1
        )
    )
    prior_state = prior[: group * head_dim].reshape(own_state.shape)
    prior_norm = prior[group * head_dim :]
    gate = jax.nn.sigmoid(mix)
    return local_part(q_parts, k, v, before, earlier, feat_q, feat_k, prior_state, prior_norm, gate)


def solution(mesh):
    return jax.shard_map(
        body,
        mesh=mesh,
        in_specs=(
            P(("heads", "seq"), None),
            P(("heads", "seq"), None),
            P(("heads", "seq"), None),
            P("heads", None, None),
            P("heads", None, None),
            P("heads"),
        ),
        out_specs=P("seq", "heads"),
        check_vma=False,
    )
```

```python
import functools

import jax
import jax.numpy as jnp
from jax import lax
from jax.experimental import pallas as pl
from jax.experimental.pallas import tpu as pltpu
from jax.sharding import PartitionSpec as P

WIN = 64
QB = 128
HEADS_PER_STEP = 2
Q_PIECES = 2
UNROLL = 8
RADIX = 4
INTERPRET = False


def passed_along(block, axis, distance):
    devices = range(lax.axis_size(axis))
    route = [(i - distance, i) for i in devices if i - distance in devices]
    return lax.ppermute(block, axis, route)


def exchange(rows, group, head_dim):
    moved = lax.all_to_all(rows, "seq", split_axis=1, concat_axis=0, tiled=True)
    return moved.reshape(group, head_dim, -1)


def feature_map(rows, weight):
    logits = jnp.einsum("hdt,hdf->htf", rows, weight, preferred_element_type=jnp.float32)
    halves = [jax.nn.softmax(logits, axis=-1), jax.nn.softmax(-logits, axis=-1)]
    return jnp.concatenate(halves, axis=-1).astype(jnp.bfloat16)


def _nt(a, b):
    return lax.dot_general(a, b, (((1,), (1,)), ((), ())), preferred_element_type=jnp.float32)


def _tn(a, b):
    return lax.dot_general(a, b, (((0,), (0,)), ((), ())), preferred_element_type=jnp.float32)


def make_kernel(t_begin, blocks):
    first = t_begin == 0

    def attend_kernel(*refs):
        (q_ref, k_ref, v_ref, pk_ref, kh_ref, vh_ref, pkh_ref, fq_ref, st_ref, z_ref, g_ref, b_ref) = refs[:12]
        if first:
            o_ref, st_out, z_out = refs[12:]
        else:
            o_ref = refs[13]
        heads = q_ref.shape[0]
        head_dim = q_ref.shape[1]
        feats = fq_ref.shape[1]
        half = feats // 2
        inv_scale = 1.0 / jnp.sqrt(jnp.float32(head_dim))
        row = lax.broadcasted_iota(jnp.int32, (feats, QB), 0)
        lo = row < half
        wk = lax.broadcasted_iota(jnp.int32, (2 * QB, QB), 0)
        tq = lax.broadcasted_iota(jnp.int32, (2 * QB, QB), 1)
        win_keep = (wk > tq + WIN) & (wk <= tq + QB)
        lin_keep = wk <= tq + WIN
        zrow = lax.broadcasted_iota(jnp.int32, (8, feats), 0)
        neg = jnp.float32(-1e30)

        def step(hh, t0, st, z, kw, vw, pkw, bias):
            q = q_ref[hh, :, pl.ds(t0 - t_begin, QB)]
            g = g_ref[hh]
            s = jnp.dot(kw, q, preferred_element_type=jnp.float32) * inv_scale
            if bias is not None:
                s = s + bias
            s = jnp.where(win_keep, s, neg)
            top = jnp.max(s, axis=0, keepdims=True)
            p = jnp.exp(s - top)
            total = jnp.sum(p, axis=0, keepdims=True)
            window = jnp.dot(vw, p.astype(jnp.bfloat16), preferred_element_type=jnp.float32)
            window = window * (1.0 / total)

            logits = jnp.dot(fq_ref[hh], q, preferred_element_type=jnp.float32)
            m_lo = jnp.max(logits[:half], axis=0, keepdims=True)
            m_hi = jnp.max(logits[half:], axis=0, keepdims=True)
            e = jnp.exp(logits - jnp.where(lo, m_lo, m_hi))
            s_lo = jnp.sum(e[:half], axis=0, keepdims=True)
            s_hi = jnp.sum(e[half:], axis=0, keepdims=True)
            phi = (e * jnp.where(lo, 1.0 / s_lo, 1.0 / s_hi)).astype(jnp.bfloat16)

            aff = jnp.dot(pkw, phi, preferred_element_type=jnp.float32)
            aff = jnp.where(lin_keep, aff, jnp.float32(0.0)).astype(jnp.bfloat16)
            num = jnp.dot(vw, aff, preferred_element_type=jnp.float32)
            den = jnp.sum(aff.astype(jnp.float32), axis=0, keepdims=True)
            st_hi = st.astype(jnp.bfloat16)
            st_lo = (st - st_hi.astype(jnp.float32)).astype(jnp.bfloat16)
            num = num + jnp.dot(st_hi, phi, preferred_element_type=jnp.float32)
            num = num + jnp.dot(st_lo, phi, preferred_element_type=jnp.float32)
            z_hi = z.astype(jnp.bfloat16)
            z_lo = (z - z_hi.astype(jnp.float32)).astype(jnp.bfloat16)
            zz = jnp.where(zrow == 0, z_hi, jnp.where(zrow == 1, z_lo, jnp.zeros_like(z_lo)))
            cross = jnp.dot(zz, phi, preferred_element_type=jnp.float32)
            den = den + (cross[0:1] + cross[1:2])
            linear = num * (1.0 / (den + 1.0))
            out = g * window + (1.0 - g) * linear
            rows = pl.ds(t0 - t_begin, QB)
            o_ref[rows, pl.ds(hh * head_dim, head_dim)] = out.T.astype(o_ref.dtype)

            vb = vw[:, :QB]
            pkb = pkw[:QB]
            st = st + jnp.dot(vb, pkb, preferred_element_type=jnp.float32)
            z = z + jnp.sum(pkb.astype(jnp.float32), axis=0, keepdims=True)
            return st, z

        carry = []
        for hh in range(heads):
            if first:
                kw0 = jnp.concatenate([kh_ref[hh], k_ref[hh, pl.ds(0, QB), :]], axis=0)
                vw0 = jnp.concatenate([vh_ref[hh], v_ref[hh, :, pl.ds(0, QB)]], axis=1)
                pkw0 = jnp.concatenate([pkh_ref[hh], pk_ref[hh, pl.ds(0, QB), :]], axis=0)
                carry.append(step(hh, 0, st_ref[hh], z_ref[hh][0:1], kw0, vw0, pkw0, b_ref[...]))
            else:
                carry.append((st_ref[hh], z_ref[hh][0:1]))

        def one(t0, carry):
            base = t0 - QB
            out = []
            for hh in range(heads):
                kw = k_ref[hh, pl.ds(base, 2 * QB), :]
                vw = v_ref[hh, :, pl.ds(base, 2 * QB)]
                pkw = pk_ref[hh, pl.ds(base, 2 * QB), :]
                out.append(step(hh, t0, carry[hh][0], carry[hh][1], kw, vw, pkw, None))
            return tuple(out)

        lo_blk = t_begin // QB + (1 if first else 0)
        hi_blk = t_begin // QB + blocks
        pairs = (hi_blk - lo_blk) // UNROLL

        def loop(i, carry):
            for u in range(UNROLL):
                t0 = pl.multiple_of((lo_blk + i * UNROLL + u) * QB, QB)
                carry = one(t0, carry)
            return carry

        final = lax.fori_loop(0, pairs, loop, tuple(carry))
        for blk in range(lo_blk + pairs * UNROLL, hi_blk):
            final = one(blk * QB, final)
        if first:
            for hh in range(heads):
                st_out[hh] = final[hh][0]
                z_out[hh] = jnp.broadcast_to(final[hh][1], (8, feats))

    return attend_kernel


def attend(q, t_begin, k_tm, v, pk, kh, vh, pkh, fq_t, st0, z0, gate_rows, bias0, prev):
    group, head_dim, span = q.shape
    length = v.shape[2]
    feats = fq_t.shape[1]
    hb = HEADS_PER_STEP
    first = prev is None
    in_specs = [
        pl.BlockSpec((hb, head_dim, span), lambda h: (h, 0, 0)),
        pl.BlockSpec((hb, length, head_dim), lambda h: (h, 0, 0)),
        pl.BlockSpec((hb, head_dim, length), lambda h: (h, 0, 0)),
        pl.BlockSpec((hb, length, feats), lambda h: (h, 0, 0)),
        pl.BlockSpec((hb, QB, head_dim), lambda h: (h, 0, 0)),
        pl.BlockSpec((hb, head_dim, QB), lambda h: (h, 0, 0)),
        pl.BlockSpec((hb, QB, feats), lambda h: (h, 0, 0)),
        pl.BlockSpec((hb, feats, head_dim), lambda h: (h, 0, 0)),
        pl.BlockSpec((hb, head_dim, feats), lambda h: (h, 0, 0)),
        pl.BlockSpec((hb, 8, feats), lambda h: (h, 0, 0)),
        pl.BlockSpec((hb, 1, QB), lambda h: (h, 0, 0)),
        pl.BlockSpec((2 * QB, QB), lambda h: (0, 0)),
    ]
    args = [q, k_tm, v, pk, kh, vh, pkh, fq_t, st0, z0, gate_rows, bias0]
    piece = t_begin // span
    out_spec = pl.BlockSpec((span, hb * head_dim), lambda h: (piece, h))
    out_shape = jax.ShapeDtypeStruct((length, group * head_dim), jnp.bfloat16)
    if first:
        out_specs = [
            out_spec,
            pl.BlockSpec((hb, head_dim, feats), lambda h: (h, 0, 0)),
            pl.BlockSpec((hb, 8, feats), lambda h: (h, 0, 0)),
        ]
        out_shapes = [
            out_shape,
            jax.ShapeDtypeStruct(st0.shape, jnp.float32),
            jax.ShapeDtypeStruct(z0.shape, jnp.float32),
        ]
        aliases = {}
    else:
        in_specs.append(pl.BlockSpec(memory_space=pl.ANY))
        args.append(prev)
        out_specs = out_spec
        out_shapes = out_shape
        aliases = {12: 0}
    return pl.pallas_call(
        make_kernel(t_begin, span // QB),
        grid=(group // hb,),
        in_specs=in_specs,
        out_specs=out_specs,
        out_shape=out_shapes,
        input_output_aliases=aliases,
        interpret=INTERPRET,
    )(*args)


def local_part(q_parts, k, k_tm, v, before, earlier, feat_q, feat_k, prior_state, prior_norm, gate):
    group, head_dim, length = k.shape
    keep = earlier.astype(jnp.bfloat16)
    phi_k = feature_map(k, feat_k)
    phi_halo = feature_map(before[0], feat_k) * keep
    halo_state = jnp.einsum(
        "htf,hdt->hdf", phi_halo, before[1], preferred_element_type=jnp.float32
    )
    halo_norm = jnp.sum(phi_halo, axis=1, dtype=jnp.float32)
    feats = phi_k.shape[2]
    pad_k = jnp.zeros((group, head_dim, QB - WIN), k.dtype)
    kh = jnp.concatenate([pad_k, before[0]], axis=2).transpose(0, 2, 1)
    vh = jnp.concatenate([pad_k, before[1]], axis=2)
    pkh = jnp.concatenate([jnp.zeros((group, QB - WIN, feats), phi_k.dtype), phi_halo], axis=1)
    fq_t = jnp.concatenate([feat_q, -feat_q], axis=2).transpose(0, 2, 1)
    st = prior_state - halo_state
    z = jnp.pad((prior_norm - halo_norm)[:, None, :], ((0, 0), (0, 7), (0, 0)))
    gate_rows = jnp.broadcast_to(gate[:, None, None], (group, 1, QB)).astype(jnp.float32)
    halo_rows = (jnp.arange(2 * QB) >= QB - WIN) & (jnp.arange(2 * QB) < QB)
    bias0 = jnp.where(halo_rows & jnp.logical_not(earlier), jnp.float32(-1e30), jnp.float32(0.0))
    bias0 = jnp.broadcast_to(bias0[:, None], (2 * QB, QB))
    span = q_parts[0].shape[2]
    out, st, z = attend(q_parts[0], 0, k_tm, v, phi_k, kh, vh, pkh, fq_t, st, z, gate_rows, bias0, None)
    for c in range(1, len(q_parts)):
        out = attend(q_parts[c], c * span, k_tm, v, phi_k, kh, vh, pkh, fq_t, st, z, gate_rows, bias0, out)
    return out


def body(queries, keys, values, feat_q, feat_k, mix):
    shards = lax.axis_size("seq")
    place = lax.axis_index("seq")
    feature_rows = queries.shape[0]
    length = queries.shape[1] // shards
    group = feat_q.shape[0]
    head_dim = feat_q.shape[1]

    halves = queries.reshape(feature_rows, shards, Q_PIECES, length // Q_PIECES).transpose(2, 1, 0, 3)
    halves, values = lax.optimization_barrier((halves, values))
    k = exchange(keys.reshape(feature_rows, shards, length), group, head_dim)
    v = exchange(values.reshape(feature_rows, shards, length), group, head_dim)
    q_parts = [
        lax.all_to_all(halves[c], "seq", split_axis=0, concat_axis=0, tiled=True).reshape(
            group, head_dim, -1
        )
        for c in range(Q_PIECES)
    ]

    earlier = place > 0
    tails = jnp.stack([k[:, :, length - WIN :], v[:, :, length - WIN :]])
    before = passed_along(tails, "seq", 1)

    phi_own = feature_map(k, feat_k)
    k_tm, phi_own = lax.optimization_barrier((k.transpose(0, 2, 1), phi_own))
    own_state = jnp.einsum("htf,hdt->hdf", phi_own, v, preferred_element_type=jnp.float32)
    own_norm = jnp.sum(phi_own, axis=1, dtype=jnp.float32)
    own = jnp.concatenate([own_state.reshape(group * head_dim, -1), own_norm], axis=0)
    prior = own
    distance = 1
    while distance < shards:
        sent = prior.astype(jnp.bfloat16)
        total = prior
        for j in range(1, RADIX):
            if distance * j < shards:
                total = total + passed_along(sent, "seq", distance * j).astype(jnp.float32)
        prior = total
        distance *= RADIX
    prior = prior - own
    prior_state = prior[: group * head_dim].reshape(own_state.shape)
    prior_norm = prior[group * head_dim :]
    gate = jax.nn.sigmoid(mix)
    return local_part(q_parts, k, k_tm, v, before, earlier, feat_q, feat_k, prior_state, prior_norm, gate)


def solution(mesh):
    return jax.shard_map(
        body,
        mesh=mesh,
        in_specs=(
            P(("heads", "seq"), None),
            P(("heads", "seq"), None),
            P(("heads", "seq"), None),
            P("heads", None, None),
            P("heads", None, None),
            P("heads"),
        ),
        out_specs=P("seq", "heads"),
        check_vma=False,
    )
```
